256 devices in a mesh: ctx: 32 (over y, x, core), head: 8 (over z).
Axes of the slice: x: 4, y: 4, z: 8, core: 2. Of those that a mesh axis runs over, the one named last changes fastest.
Arguments:
- query_vectors: bfloat16 [4096, 4096], P('ctx', 'head'), may hold values from -6 to 6
- key_vectors: bfloat16 [4096, 4096], P('ctx', 'head'), may hold values from -1.5 to 1.5
- value_vectors: bfloat16 [4096, 4096], P('ctx', 'head'), may hold values from -6 to 6
- log_decay: float32 [32, 4096], P('head', 'ctx'), may hold values from -2 to 0, as said below
- residual: bfloat16 [4096, 3072], P('ctx'), may hold values from -6 to 6
- out_weight: bfloat16 [4096, 3072], P('head', 'ctx'), may hold values from -0.09375 to 0.09375
- attn_gain: float32 [4096], P('head'), may hold values from 0.1 to 1.9
- moe_gain: float32 [3072], replicated, may hold values from 0.1 to 1.9
- router: float32 [3072, 32], replicated, may hold values from -0.109375 to 0.109375
- w_gate: bfloat16 [32, 3072, 4608], P('ctx', None, 'head'), may hold values from -0.109375 to 0.109375
- w_up: bfloat16 [32, 3072, 4608], P('ctx', None, 'head'), may hold values from -0.109375 to 0.109375
- w_down: bfloat16 [32, 4608, 3072], P('ctx', 'head'), may hold values from -0.09375 to 0.09375
- expert_ids: int32 [4096, 2], P('ctx'), may hold values from 0 to 31, all different within a row; in each aligned block of 128 rows (0 to 127, 128 to 255, ...) at most 16 rows name the same one
Outputs:
- final_out: bfloat16 [4096, 3072], P('ctx', 'head')
The draws below stay inside these ranges and needn't reach their ends.
Inputs may be any that keep to these rules, and one draw needn't show every extreme that they name: `expert_ids`: each row names 2 different experts. In each aligned block of 128 rows no expert is named by more than 16 rows, and in every draw some expert is named by exactly 16 rows of some block. `log_decay`: every entry is negative.
All inputs are finite; a program needn't handle non-finite values.
Results may differ from the reference program's by a relative error of at most 0.022.
Values may be sent and summed in bfloat16 or wider, within the bound.
No kernel may reach another device: no remote copies, remote signals or barrier semaphores. Data moves between devices by JAX's collectives and lax.ppermute only.
A program may use at most 128 MiB of HBM per device.

```python
import math
from functools import partial
import jax
import jax.numpy as jnp
import numpy as np
from jax import lax

D = 3072
HEAD_COUNT = 32
HDIM = 128
FF = 4608
TOP = 2
TOK_DEV = 128
EXPERTS = 32
CAP = 16
SEQUENCE_LENGTH = 4096
N_HEAD = 8


def draw_log_decay(key, part):
    random_keys = jax.random.split(key, 7)
    fast_share = 0.5
    fast_heads = jax.random.uniform(random_keys[0], (HEAD_COUNT, 1)) < fast_share
    fast_rate = jnp.exp(jax.random.uniform(random_keys[1], (HEAD_COUNT, 1), minval=math.log(1.0 / 50.0), maxval=math.log(1.0 / 30.0)))
    slow_rate = jnp.exp(jax.random.uniform(random_keys[2], (HEAD_COUNT, 1), minval=math.log(0.2), maxval=math.log(0.8))) / SEQUENCE_LENGTH
    baseline_decay = jnp.where(fast_heads, fast_rate, slow_rate)
    blocks_total = SEQUENCE_LENGTH // TOK_DEV
    block_factor = jnp.exp(jax.random.uniform(random_keys[3], (HEAD_COUNT, blocks_total, 1), minval=math.log(0.5), maxval=math.log(2.0)))
    block_factor = jnp.broadcast_to(block_factor, (HEAD_COUNT, blocks_total, TOK_DEV)).reshape(HEAD_COUNT, SEQUENCE_LENGTH)
    jitter_amount = jax.random.uniform(random_keys[4], (HEAD_COUNT, SEQUENCE_LENGTH), minval=0.5, maxval=1.5)
    spike_positions = jax.random.randint(random_keys[5], (HEAD_COUNT, 2), 0, SEQUENCE_LENGTH)
    spike_magnitude = jax.random.uniform(random_keys[6], (HEAD_COUNT, 2), minval=math.log(0.5), maxval=math.log(0.8))
    position_index = jax.lax.broadcasted_iota(jnp.int32, (HEAD_COUNT, SEQUENCE_LENGTH, 2), 1)
    spike_events = jnp.sum(jnp.where(position_index == spike_positions[:, None, :], spike_magnitude[:, None, :], 0.0), axis=2)
    return (-(baseline_decay * block_factor * jitter_amount) + spike_events).astype(jnp.float32)


def levels(own_key, extent, pieces, low, top_value):
    def one(dim, blocks):
        heights = jax.random.uniform(jax.random.fold_in(jax.random.fold_in(own_key, 6), dim), (blocks,), jnp.float32, low / len(pieces), top_value / len(pieces))
        return jnp.repeat(jnp.exp(heights), extent[dim] // blocks).reshape((-1,) + (1,) * (len(extent) - dim - 1))

    gain = one(*pieces[0])
    for cut in pieces[1:]:
        gain = gain * one(*cut)
    return gain


def routed_block(stream_key, own, number, rows, number_of, top, reach, skew):
    ranking = jax.random.permutation(stream_key, number_of)
    heavy_load, common = portions_of(number_of, rows * top, reach, skew, True), portions_of(number_of, rows * top, reach, skew, False)
    places = jnp.arange(number_of)

    def named(sizes, offset_by):
        used = int((sizes > 0).sum())
        fixed = max(1, used // 4)
        moved = fixed + (places - fixed + offset_by * (used - fixed)) % max(1, number_of - fixed)
        return jnp.zeros((number_of,), jnp.int32).at[ranking[jnp.where(places < fixed, places, moved)]].set(jnp.asarray(sizes, jnp.int32))

    sizes = jnp.where(number % 4 == 0, named(heavy_load, number // 4), named(common, number - number // 4 - 1))
    mixed = jax.random.permutation(jax.random.fold_in(own, 3), number_of)
    giver, sink = mixed[0:number_of // 2 * 2:2], mixed[1:number_of // 2 * 2:2]
    margin = jnp.minimum(sizes[giver] - 1, reach - sizes[sink]) // 2
    margin = jnp.where((giver == ranking[0]) | (sink == ranking[0]) | (sizes[sink] == 0), 0, jnp.maximum(margin, 0))
    moved = jax.random.randint(jax.random.fold_in(own, 4), (number_of // 2,), 0, 1 << 20) % (margin + 1)
    sizes = sizes.at[giver].add(-moved).at[sink].add(moved)
    labels = jnp.searchsorted(jnp.cumsum(sizes), jnp.arange(rows * top), side="right").astype(jnp.int32)
    table = labels.reshape(top, rows).T
    table = table[jax.random.permutation(jax.random.fold_in(own, 1), rows)]
    offset_by = jax.random.randint(jax.random.fold_in(own, 2), (rows, 1), 0, top)
    return jnp.take_along_axis(table, (jnp.arange(top)[None, :] + offset_by) % top, axis=1)


def portions_of(amount, total, bound, slope, full):
    portions = [(1 << 20) // math.isqrt(rank ** slope) + 1 for rank in range(1, amount + 1)]
    largest = bound if full else min(bound, max(-(-total // amount), total * portions[0] // sum(portions)))
    least = 1 if total - largest >= amount - 1 else 0
    given, rest = [largest] + [least] * (amount - 1), total - largest - least * (amount - 1)
    while rest > 0:
        candidates = [i for i in range(1, amount) if given[i] < largest] or [i for i in range(1, amount) if given[i] < bound]
        pool, budget = sum([portions[i] for i in candidates]), rest
        for i in candidates:
            more = min(bound - given[i], max(1, budget * portions[i] // pool), rest)
            given[i] = given[i] + more
            rest = rest - more
    return np.array(given)


def bell_draw(stream_key, dims, deviation, reach, cuts=(), held_as=jnp.bfloat16):
    loudness = levels(stream_key, dims, cuts, -0.22, 0.18) if cuts else 1.0
    drawn = jax.random.normal(stream_key, dims, jnp.float32) * deviation * loudness
    return jnp.minimum(jnp.maximum(drawn, -reach), reach).astype(held_as)


def setup_inputs(seed: int = 0) -> dict:
    arg_keys = jax.random.split(jax.random.key(seed), 14)
    query_vectors = bell_draw(arg_keys[0], (SEQUENCE_LENGTH, HEAD_COUNT * HDIM), 1.0, 6.0, ((0, 32), (1, 8)))
    key_vectors = bell_draw(arg_keys[1], (SEQUENCE_LENGTH, HEAD_COUNT * HDIM), 0.25, 1.5, ((0, 32), (1, 8)))
    value_vectors = bell_draw(arg_keys[2], (SEQUENCE_LENGTH, HEAD_COUNT * HDIM), 1.0, 6.0, ((0, 32), (1, 8)))
    log_decay = draw_log_decay(jax.random.fold_in(arg_keys[13], 71), 0)
    residual = bell_draw(arg_keys[4], (SEQUENCE_LENGTH, D), 1.0, 6.0, ((0, 32),))
    out_weight = bell_draw(arg_keys[5], (HEAD_COUNT * HDIM, D), (HEAD_COUNT * HDIM) ** -0.5, 0.09375, ((0, 8), (1, 32)))
    attn_gain = jnp.clip(1.0 + 0.18 * jax.random.normal(arg_keys[6], (HEAD_COUNT * HDIM,), jnp.float32), 0.1, 1.9)
    moe_gain = jnp.clip(1.0 + 0.18 * jax.random.normal(arg_keys[7], (D,), jnp.float32), 0.1, 1.9)
    router = bell_draw(arg_keys[8], (D, EXPERTS), D ** -0.5, 0.109375, (), jnp.float32)
    w_gate = bell_draw(arg_keys[9], (EXPERTS, D, FF), D ** -0.5, 0.109375, ((0, 32), (2, 8)))
    w_up = bell_draw(arg_keys[10], (EXPERTS, D, FF), D ** -0.5, 0.109375, ((0, 32), (2, 8)))
    w_down = bell_draw(arg_keys[11], (EXPERTS, FF, D), FF ** -0.5, 0.09375, ((0, 32), (1, 8)))
    expert_ids_keys = jax.random.split(jax.random.fold_in(arg_keys[12], 1), SEQUENCE_LENGTH // TOK_DEV)
    expert_ids_turns = jax.random.permutation(jax.random.fold_in(arg_keys[12], 3), SEQUENCE_LENGTH // TOK_DEV)
    expert_ids = jax.vmap(lambda own, number: routed_block(jax.random.fold_in(arg_keys[12], 2), own, number, TOK_DEV, EXPERTS, TOP, CAP, 2))(expert_ids_keys, expert_ids_turns).reshape((SEQUENCE_LENGTH, TOP))
    return dict(query_vectors=query_vectors, key_vectors=key_vectors, value_vectors=value_vectors, log_decay=log_decay, residual=residual, out_weight=out_weight, attn_gain=attn_gain, moe_gain=moe_gain, router=router, w_gate=w_gate, w_up=w_up, w_down=w_down, expert_ids=expert_ids)


PRECISE = lax.Precision.HIGHEST

def block_attention(query_block, key_block, value_block, decay_block, state_before):
    running = jnp.cumsum(decay_block, axis=1)
    length_here = decay_block.shape[1]
    row_index = lax.broadcasted_iota(jnp.int32, (length_here, length_here), 0)
    col_index = lax.broadcasted_iota(jnp.int32, (length_here, length_here), 1)
    causal = (col_index <= row_index)[None]
    spread = jnp.where(causal, running[:, :, None] - running[:, None, :], 0.0)
    decay_weights = jnp.where(causal, jnp.exp(spread), 0.0)
    scores = jnp.einsum('htd,hsd->hts', query_block, key_block, precision=PRECISE) * decay_weights
    inside_part = jnp.einsum('hts,hse->hte', scores, value_block, precision=PRECISE)
    outside_part = jnp.exp(running)[:, :, None] * jnp.einsum('htd,hde->hte', query_block, state_before, precision=PRECISE)
    final_log = running[:, -1]
    tail_decay = jnp.exp(final_log[:, None] - running)
    local_state = jnp.einsum('hsd,hse->hde', key_block * tail_decay[:, :, None], value_block, precision=PRECISE)
    state_after = jnp.exp(final_log)[:, None, None] * state_before + local_state
    return (inside_part + outside_part, state_after)

def route_tokens(logits, expert_ids, experts_total):
    onehot = expert_ids[:, :, None] == lax.broadcasted_iota(jnp.int32, (1, 1, experts_total), 2)
    chosen = lax.optimization_barrier(jnp.sum(jnp.where(onehot, logits[:, None, :], 0.0), axis=2))
    leading = jax.nn.sigmoid(chosen[:, 0] - chosen[:, 1])
    gate_weights = jnp.stack([leading, 1.0 - leading], axis=1)
    marked = onehot.reshape(-1, experts_total).astype(jnp.int32)
    earlier = jnp.cumsum(marked, axis=0) - marked
    slot_index = lax.optimization_barrier(jnp.sum(earlier * marked, axis=1)).reshape(expert_ids.shape).astype(jnp.int32)
    return (gate_weights, slot_index)

def reference(query_vectors, key_vectors, value_vectors, log_decay, residual, out_weight, attn_gain, moe_gain, router, w_gate, w_up, w_down, expert_ids):
    blocks_total = SEQUENCE_LENGTH // TOK_DEV

    def split_heads(matrix_in):
        return matrix_in.astype(jnp.float32).reshape(blocks_total, TOK_DEV, HEAD_COUNT, HDIM).transpose(0, 2, 1, 3)
    decays = log_decay.reshape(HEAD_COUNT, blocks_total, TOK_DEV).transpose(1, 0, 2)

    def advance(state_now, inputs):
        attended, state_next = block_attention(inputs[0], inputs[1], inputs[2], inputs[3], state_now)
        return (state_next, attended)
    initial = jnp.zeros((HEAD_COUNT, HDIM, HDIM), jnp.float32)
    _, attended = lax.scan(advance, initial, (split_heads(query_vectors), split_heads(key_vectors), split_heads(value_vectors), decays))
    attended = attended.transpose(0, 2, 1, 3).reshape(SEQUENCE_LENGTH, HEAD_COUNT, HDIM)
    square_mean = lax.optimization_barrier(jnp.mean(attended * attended, axis=2, keepdims=True))
    heads_normed = (attended * lax.rsqrt(square_mean + 1e-05) * attn_gain.reshape(1, HEAD_COUNT, HDIM)).astype(jnp.bfloat16)
    heads_normed = heads_normed.reshape(SEQUENCE_LENGTH, HEAD_COUNT * HDIM)
    projected = jnp.dot(heads_normed, out_weight, preferred_element_type=jnp.float32)
    mixed_rows = (residual.astype(jnp.float32) + projected).astype(jnp.bfloat16)
    mixed_wide = mixed_rows.astype(jnp.float32)
    inv_rms = lax.rsqrt(lax.optimization_barrier(jnp.mean(mixed_wide * mixed_wide, axis=1, keepdims=True)) + 1e-06)
    scaled = mixed_wide * moe_gain[None, :]
    moe_in = (scaled * inv_rms).astype(jnp.bfloat16)
    logits = inv_rms * jnp.dot(scaled, router, precision=PRECISE)
    ids_blocks = expert_ids.reshape(blocks_total, TOK_DEV, TOP).astype(jnp.int32)
    gate_weights, slot_index = jax.vmap(partial(route_tokens, experts_total=EXPERTS))(logits.reshape(blocks_total, TOK_DEV, EXPERTS), ids_blocks)
    block_number = lax.broadcasted_iota(jnp.int32, (blocks_total, TOK_DEV, TOP), 0)
    token_number = block_number * TOK_DEV + lax.broadcasted_iota(jnp.int32, (blocks_total, TOK_DEV, TOP), 1)
    row_table = jnp.full((EXPERTS, blocks_total, CAP), SEQUENCE_LENGTH, jnp.int32)
    row_table = row_table.at[ids_blocks, block_number, slot_index].set(token_number)
    padded_in = jnp.concatenate([moe_in, jnp.zeros((1, D), jnp.bfloat16)], axis=0)
    group_width = FF // N_HEAD

    def run_expert(inputs):
        index_rows, gate_matrix, up_matrix, down_matrix = inputs
        gathered = padded_in[index_rows.reshape(-1)]
        hidden = (jax.nn.silu(jnp.dot(gathered, gate_matrix, preferred_element_type=jnp.float32)) * jnp.dot(gathered, up_matrix, preferred_element_type=jnp.float32)).astype(jnp.bfloat16)
        summed = jnp.zeros((gathered.shape[0], D), jnp.float32)
        for group_index in range(N_HEAD):
            lower_edge = group_index * group_width
            partial_sum = jnp.dot(hidden[:, lower_edge:lower_edge + group_width], down_matrix[lower_edge:lower_edge + group_width], preferred_element_type=jnp.float32)
            partial_sum = lax.optimization_barrier(partial_sum.astype(jnp.bfloat16))
            summed = summed + partial_sum.astype(jnp.float32)
        return summed.astype(jnp.bfloat16)
    expert_out = lax.map(run_expert, (row_table, w_gate, w_up, w_down))
    flat_out = expert_out.reshape(EXPERTS * blocks_total * CAP, D)
    pick_index = (ids_blocks * (blocks_total * CAP) + block_number * CAP + slot_index).reshape(SEQUENCE_LENGTH, TOP).astype(jnp.int32)
    picked = flat_out[pick_index].astype(jnp.float32)
    gate_flat = gate_weights.reshape(SEQUENCE_LENGTH, TOP)
    final_out = mixed_wide + gate_flat[:, 0:1] * picked[:, 0] + gate_flat[:, 1:2] * picked[:, 1]
    return final_out.astype(jnp.bfloat16)
```

```python
import jax
import jax.numpy as jnp
from jax import lax
from jax.sharding import PartitionSpec as P

TOP = 2


PRECISE = lax.Precision.HIGHEST


def prior_states(final_log, local_state, axis):
    index = lax.axis_index(axis)
    totals = lax.all_gather(final_log, axis)
    states = lax.all_gather(local_state.astype(jnp.bfloat16), axis)
    peers = totals.shape[0]
    source = lax.broadcasted_iota(jnp.int32, (peers, peers), 0)
    between = lax.broadcasted_iota(jnp.int32, (peers, peers), 1)
    inside = (between > source) & (between < index)
    spans = jnp.sum(jnp.where(inside[:, :, None], totals[None, :, :], 0.0), axis=1)
    weights = jnp.where(jnp.arange(peers)[:, None] < index, jnp.exp(spans), 0.0)
    return jnp.einsum(
        "jh,jhde->hde", weights, states.astype(jnp.float32), precision=PRECISE
    )


def local_attention(query_block, key_block, value_block, decay_block):
    running = jnp.cumsum(decay_block, axis=1)
    length_here = decay_block.shape[1]
    row_index = lax.broadcasted_iota(jnp.int32, (length_here, length_here), 0)
    col_index = lax.broadcasted_iota(jnp.int32, (length_here, length_here), 1)
    causal = (col_index <= row_index)[None]
    spread = jnp.where(causal, running[:, :, None] - running[:, None, :], 0.0)
    decay_weights = jnp.where(causal, jnp.exp(spread), 0.0)
    scores = jnp.einsum("htd,hsd->hts", query_block, key_block, precision=PRECISE) * decay_weights
    inside_part = jnp.einsum("hts,hse->hte", scores, value_block, precision=PRECISE)
    final_log = running[:, -1]
    tail_decay = jnp.exp(final_log[:, None] - running)
    local_state = jnp.einsum(
        "hsd,hse->hde", key_block * tail_decay[:, :, None], value_block, precision=PRECISE
    )
    return (inside_part, running, local_state, final_log)


def route_tokens(logits, expert_ids, experts_total):
    onehot = expert_ids[:, :, None] == lax.broadcasted_iota(jnp.int32, (1, 1, experts_total), 2)
    chosen = jnp.sum(jnp.where(onehot, logits[:, None, :], 0.0), axis=2)
    leading = jax.nn.sigmoid(chosen[:, 0] - chosen[:, 1])
    gate_weights = jnp.stack([leading, 1.0 - leading], axis=1)
    marked = onehot.reshape(-1, experts_total).astype(jnp.int32)
    earlier = jnp.cumsum(marked, axis=0) - marked
    slot_index = jnp.sum(earlier * marked, axis=1).reshape(expert_ids.shape)
    return (gate_weights, slot_index)


def body(
    query_vectors,
    key_vectors,
    value_vectors,
    log_decay,
    residual,
    out_weight,
    attn_gain,
    moe_gain,
    router,
    w_gate,
    w_up,
    w_down,
    expert_ids,
):
    token_count = query_vectors.shape[0]
    heads_here = log_decay.shape[0]
    head_size = query_vectors.shape[1] // heads_here

    def split_heads(matrix_in):
        return (
            matrix_in.astype(jnp.float32)
            .reshape(token_count, heads_here, head_size)
            .transpose(1, 0, 2)
        )

    query_heads = split_heads(query_vectors)
    inside_part, running, local_state, final_log = local_attention(
        query_heads, split_heads(key_vectors), split_heads(value_vectors), log_decay
    )
    prior_state = prior_states(final_log, local_state, "ctx")
    outside_part = jnp.exp(running)[:, :, None] * jnp.einsum(
        "htd,hde->hte", query_heads, prior_state, precision=PRECISE
    )
    attended = inside_part + outside_part
    square_mean = jnp.mean(attended * attended, axis=2, keepdims=True)
    heads_normed = (
        attended * lax.rsqrt(square_mean + 1e-05) * attn_gain.reshape(heads_here, 1, head_size)
    )
    heads_normed = (
        heads_normed.astype(jnp.bfloat16)
        .transpose(1, 0, 2)
        .reshape(token_count, heads_here * head_size)
    )
    partial_out = jnp.dot(
        heads_normed,
        lax.all_gather(out_weight, "ctx", axis=1, tiled=True),
        preferred_element_type=jnp.float32,
    )
    model_width = residual.shape[1]
    experts_total = router.shape[1]
    capacity = 2 * token_count * TOP // experts_total
    slice_width = model_width // lax.axis_size("head")
    slice_start = lax.axis_index("head") * slice_width
    projected = lax.psum(partial_out.astype(jnp.bfloat16), "head").astype(jnp.float32)
    mixed_rows = (residual.astype(jnp.float32) + projected).astype(jnp.bfloat16)
    mixed_wide = mixed_rows.astype(jnp.float32)
    inv_rms = lax.rsqrt(jnp.mean(mixed_wide * mixed_wide, axis=1, keepdims=True) + 1e-06)
    scaled = mixed_wide * moe_gain[None, :]
    moe_in = (scaled * inv_rms).astype(jnp.bfloat16)
    logits = inv_rms * jnp.dot(scaled, router, precision=PRECISE)
    base_slice = lax.dynamic_slice_in_dim(mixed_wide, slice_start, slice_width, 1)
    gate_weights, slot_index = route_tokens(logits, expert_ids, experts_total)
    target = (expert_ids * capacity + slot_index).reshape(-1)
    width_here = moe_in.shape[1]
    source = jnp.repeat(moe_in, TOP, axis=0)
    packed = jnp.zeros((experts_total * capacity, width_here), jnp.bfloat16).at[target].set(source)
    arrived = lax.all_to_all(
        packed.reshape(experts_total, capacity, width_here),
        "ctx",
        split_axis=0,
        concat_axis=0,
        tiled=True,
    )
    flat_rows = arrived.reshape(-1, model_width)
    gate_part = jnp.dot(flat_rows, w_gate[0], preferred_element_type=jnp.float32)
    up_part = jnp.dot(flat_rows, w_up[0], preferred_element_type=jnp.float32)
    hidden = (jax.nn.silu(gate_part) * up_part).astype(jnp.bfloat16)
    partial_down = jnp.dot(hidden, w_down[0], preferred_element_type=jnp.float32)
    summed = lax.psum_scatter(
        partial_down.astype(jnp.bfloat16), "head", scatter_dimension=1, tiled=True
    )
    returned = lax.all_to_all(
        summed.reshape(experts_total, capacity, slice_width),
        "ctx",
        split_axis=0,
        concat_axis=0,
        tiled=True,
    )
    lookup = returned.reshape(experts_total * capacity, slice_width)
    picked = lookup[target].reshape(token_count, TOP, slice_width).astype(jnp.float32)
    final_out = (
        base_slice + gate_weights[:, 0:1] * picked[:, 0] + gate_weights[:, 1:2] * picked[:, 1]
    )
    return final_out.astype(jnp.bfloat16)


def solution(mesh):
    in_specs = (
        P("ctx", "head"),
        P("ctx", "head"),
        P("ctx", "head"),
        P("head", "ctx"),
        P("ctx", None),
        P("head", "ctx"),
        P("head"),
        P(),
        P(),
        P("ctx", None, "head"),
        P("ctx", None, "head"),
        P("ctx", "head", None),
        P("ctx", None),
    )
    out_specs = P("ctx", "head")
    return jax.shard_map(body, mesh=mesh, in_specs=in_specs, out_specs=out_specs, check_vma=False)
```

```python
import jax
import jax.numpy as jnp
from jax import lax
from jax.sharding import PartitionSpec as P

TOP = 2


PRECISE = lax.Precision.HIGHEST


def prior_states(final_log, local_state, axis):
    index = lax.axis_index(axis)
    heads_here, head_size = local_state.shape[0], local_state.shape[2]
    high = final_log.astype(jnp.bfloat16)
    rest = final_log - high.astype(jnp.float32)
    middle = rest.astype(jnp.bfloat16)
    low = (rest - middle.astype(jnp.float32)).astype(jnp.bfloat16)
    extra = jnp.zeros((heads_here, 16, head_size), jnp.bfloat16)
    extra = extra.at[:, 0:3, 0].set(jnp.stack([high, middle, low], axis=1))
    packed = jnp.concatenate([local_state.astype(jnp.bfloat16), extra], axis=1)
    gathered = lax.all_gather(packed, axis)
    states = gathered[:, :, :head_size]
    totals = jnp.sum(gathered[:, :, head_size : head_size + 3, 0].astype(jnp.float32), axis=2)
    peers = totals.shape[0]
    source = lax.broadcasted_iota(jnp.int32, (peers, peers), 0)
    between = lax.broadcasted_iota(jnp.int32, (peers, peers), 1)
    inside = (between > source) & (between < index)
    spans = jnp.sum(jnp.where(inside[:, :, None], totals[None, :, :], 0.0), axis=1)
    weights = jnp.where(jnp.arange(peers)[:, None] < index, jnp.exp(spans), 0.0)
    return jnp.einsum(
        "jh,jhde->hde", weights, states.astype(jnp.float32), precision=PRECISE
    )


def local_attention(query_block, key_block, value_block, decay_block):
    running = jnp.cumsum(decay_block, axis=1)
    length_here = decay_block.shape[1]
    row_index = lax.broadcasted_iota(jnp.int32, (length_here, length_here), 0)
    col_index = lax.broadcasted_iota(jnp.int32, (length_here, length_here), 1)
    causal = (col_index <= row_index)[None]
    spread = jnp.where(causal, running[:, :, None] - running[:, None, :], 0.0)
    decay_weights = jnp.where(causal, jnp.exp(spread), 0.0)
    scores = jnp.einsum("htd,hsd->hts", query_block, key_block, precision=PRECISE) * decay_weights
    inside_part = jnp.einsum("hts,hse->hte", scores, value_block, precision=PRECISE)
    final_log = running[:, -1]
    tail_decay = jnp.exp(final_log[:, None] - running)
    local_state = jnp.einsum(
        "hsd,hse->hde", key_block * tail_decay[:, :, None], value_block, precision=PRECISE
    )
    return (inside_part, running, local_state, final_log)


def route_tokens(logits, expert_ids, experts_total):
    onehot = expert_ids[:, :, None] == lax.broadcasted_iota(jnp.int32, (1, 1, experts_total), 2)
    chosen = jnp.sum(jnp.where(onehot, logits[:, None, :], 0.0), axis=2)
    leading = jax.nn.sigmoid(chosen[:, 0] - chosen[:, 1])
    gate_weights = jnp.stack([leading, 1.0 - leading], axis=1)
    marked = onehot.reshape(-1, experts_total).astype(jnp.int32)
    earlier = jnp.cumsum(marked, axis=0) - marked
    slot_index = jnp.sum(earlier * marked, axis=1).reshape(expert_ids.shape)
    return (gate_weights, slot_index)


def body(
    query_vectors,
    key_vectors,
    value_vectors,
    log_decay,
    residual,
    out_weight,
    attn_gain,
    moe_gain,
    router,
    w_gate,
    w_up,
    w_down,
    expert_ids,
):
    token_count = query_vectors.shape[0]
    heads_here = log_decay.shape[0]
    head_size = query_vectors.shape[1] // heads_here

    def split_heads(matrix_in):
        return (
            matrix_in.astype(jnp.float32)
            .reshape(token_count, heads_here, head_size)
            .transpose(1, 0, 2)
        )

    query_heads = split_heads(query_vectors)
    inside_part, running, local_state, final_log = local_attention(
        query_heads, split_heads(key_vectors), split_heads(value_vectors), log_decay
    )
    prior_state = prior_states(final_log, local_state, "ctx")
    outside_part = jnp.exp(running)[:, :, None] * jnp.einsum(
        "htd,hde->hte", query_heads, prior_state, precision=PRECISE
    )
    attended = inside_part + outside_part
    square_mean = jnp.mean(attended * attended, axis=2, keepdims=True)
    heads_normed = (
        attended * lax.rsqrt(square_mean + 1e-05) * attn_gain.reshape(heads_here, 1, head_size)
    )
    heads_normed = (
        heads_normed.astype(jnp.bfloat16)
        .transpose(1, 0, 2)
        .reshape(token_count, heads_here * head_size)
    )
    ctx_size = lax.axis_size("ctx")
    head_count = lax.axis_size("head")
    weight_blocks = lax.all_to_all(
        jnp.broadcast_to(out_weight[None], (ctx_size,) + out_weight.shape),
        "ctx",
        split_axis=0,
        concat_axis=0,
        tiled=True,
    )
    model_width = residual.shape[1]
    experts_total = router.shape[1]
    capacity = 2 * token_count * TOP // experts_total
    slice_width = model_width // head_count
    slice_start = lax.axis_index("head") * slice_width
    partial_out = jnp.einsum(
        "tk,ckd->tcd", heads_normed, weight_blocks, preferred_element_type=jnp.float32
    ).reshape(token_count, head_count, slice_width)
    pieces = lax.all_to_all(
        partial_out.astype(jnp.bfloat16).transpose(1, 0, 2),
        "head",
        split_axis=0,
        concat_axis=0,
        tiled=True,
    )
    projected = jnp.sum(pieces.astype(jnp.float32), axis=0)
    own_residual = lax.dynamic_slice_in_dim(residual, slice_start, slice_width, 1)
    mixed_slice = (own_residual.astype(jnp.float32) + projected).astype(jnp.bfloat16)
    mixed_all = lax.all_to_all(
        jnp.broadcast_to(mixed_slice[None], (head_count,) + mixed_slice.shape),
        "head",
        split_axis=0,
        concat_axis=0,
        tiled=True,
    )
    mixed_rows = mixed_all.transpose(1, 0, 2).reshape(token_count, model_width)
    mixed_wide = mixed_rows.astype(jnp.float32)
    inv_rms = lax.rsqrt(jnp.mean(mixed_wide * mixed_wide, axis=1, keepdims=True) + 1e-06)
    scaled = mixed_wide * moe_gain[None, :]
    moe_in = (scaled * inv_rms).astype(jnp.bfloat16)
    logits = inv_rms * jnp.dot(scaled, router, precision=PRECISE)
    base_slice = lax.dynamic_slice_in_dim(mixed_wide, slice_start, slice_width, 1)
    gate_weights, slot_index = route_tokens(logits, expert_ids, experts_total)
    target = (expert_ids * capacity + slot_index).reshape(-1)
    width_here = moe_in.shape[1]
    source = jnp.repeat(moe_in, TOP, axis=0)
    packed = jnp.zeros((experts_total * capacity, width_here), jnp.bfloat16).at[target].set(source)
    arrived = lax.all_to_all(
        packed.reshape(experts_total, capacity, width_here),
        "ctx",
        split_axis=0,
        concat_axis=0,
        tiled=True,
    )
    flat_rows = arrived.reshape(-1, model_width)
    gate_part = jnp.dot(flat_rows, w_gate[0], preferred_element_type=jnp.float32)
    up_part = jnp.dot(flat_rows, w_up[0], preferred_element_type=jnp.float32)
    hidden = (jax.nn.silu(gate_part) * up_part).astype(jnp.bfloat16)
    partial_down = jnp.dot(hidden, w_down[0], preferred_element_type=jnp.float32)
    summed = lax.psum_scatter(
        partial_down.astype(jnp.bfloat16), "head", scatter_dimension=1, tiled=True
    )
    returned = lax.all_to_all(
        summed.reshape(experts_total, capacity, slice_width),
        "ctx",
        split_axis=0,
        concat_axis=0,
        tiled=True,
    )
    lookup = returned.reshape(experts_total * capacity, slice_width)
    picked = lookup[target].reshape(token_count, TOP, slice_width).astype(jnp.float32)
    final_out = (
        base_slice + gate_weights[:, 0:1] * picked[:, 0] + gate_weights[:, 1:2] * picked[:, 1]
    )
    return final_out.astype(jnp.bfloat16)


def solution(mesh):
    in_specs = (
        P("ctx", "head"),
        P("ctx", "head"),
        P("ctx", "head"),
        P("head", "ctx"),
        P("ctx", None),
        P("head", "ctx"),
        P("head"),
        P(),
        P(),
        P("ctx", None, "head"),
        P("ctx", None, "head"),
        P("ctx", "head", None),
        P("ctx", None),
    )
    out_specs = P("ctx", "head")
    return jax.shard_map(body, mesh=mesh, in_specs=in_specs, out_specs=out_specs, check_vma=False)
```

```python
import jax
import jax.numpy as jnp
from jax import lax
from jax.sharding import PartitionSpec as P

TOP = 2


PRECISE = lax.Precision.HIGHEST


def prior_states(final_log, local_state, axis):
    peers = lax.axis_size(axis)
    heads_here, head_size = local_state.shape[0], local_state.shape[2]
    totals = jnp.broadcast_to(final_log[:, None, None], (heads_here, 8, head_size))
    packed = jnp.concatenate([local_state, totals], axis=1)
    row = lax.broadcasted_iota(jnp.int32, packed.shape, 1)

    def combine(earlier, later):
        scale = jnp.exp(later[:, head_size : head_size + 1, 0:1])
        return later + jnp.where(row < head_size, scale, 1.0) * earlier

    def shifted(value, distance):
        pairs = [(k, k + distance) for k in range(peers - distance)]
        return lax.ppermute(value, axis, pairs)

    before = combine(shifted(packed, 2), shifted(packed, 1))
    distance = 2
    while distance < peers:
        before = combine(shifted(before, distance), before)
        distance *= 2
    return before[:, :head_size]


def local_attention(query_block, key_block, value_block, decay_block):
    running = jnp.cumsum(decay_block, axis=1)
    length_here = decay_block.shape[1]
    row_index = lax.broadcasted_iota(jnp.int32, (length_here, length_here), 0)
    col_index = lax.broadcasted_iota(jnp.int32, (length_here, length_here), 1)
    causal = (col_index <= row_index)[None]
    spread = jnp.where(causal, running[:, :, None] - running[:, None, :], 0.0)
    decay_weights = jnp.where(causal, jnp.exp(spread), 0.0)
    scores = jnp.einsum("htd,hsd->hts", query_block, key_block, precision=PRECISE) * decay_weights
    inside_part = jnp.einsum("hts,hse->hte", scores, value_block, precision=PRECISE)
    final_log = running[:, -1]
    tail_decay = jnp.exp(final_log[:, None] - running)
    local_state = jnp.einsum(
        "hsd,hse->hde", key_block * tail_decay[:, :, None], value_block, precision=PRECISE
    )
    return (inside_part, running, local_state, final_log)


def route_tokens(logits, expert_ids, experts_total):
    onehot = expert_ids[:, :, None] == lax.broadcasted_iota(jnp.int32, (1, 1, experts_total), 2)
    chosen = jnp.sum(jnp.where(onehot, logits[:, None, :], 0.0), axis=2)
    leading = jax.nn.sigmoid(chosen[:, 0] - chosen[:, 1])
    gate_weights = jnp.stack([leading, 1.0 - leading], axis=1)
    marked = onehot.reshape(-1, experts_total).astype(jnp.int32)
    earlier = jnp.cumsum(marked, axis=0) - marked
    slot_index = jnp.sum(earlier * marked, axis=1).reshape(expert_ids.shape)
    return (gate_weights, slot_index)


def body(
    query_vectors,
    key_vectors,
    value_vectors,
    log_decay,
    residual,
    out_weight,
    attn_gain,
    moe_gain,
    router,
    w_gate,
    w_up,
    w_down,
    expert_ids,
):
    token_count = query_vectors.shape[0]
    heads_here = log_decay.shape[0]
    head_size = query_vectors.shape[1] // heads_here

    def split_heads(matrix_in):
        return (
            matrix_in.astype(jnp.float32)
            .reshape(token_count, heads_here, head_size)
            .transpose(1, 0, 2)
        )

    query_heads = split_heads(query_vectors)
    inside_part, running, local_state, final_log = local_attention(
        query_heads, split_heads(key_vectors), split_heads(value_vectors), log_decay
    )
    prior_state = prior_states(final_log, local_state, "ctx")
    outside_part = jnp.exp(running)[:, :, None] * jnp.einsum(
        "htd,hde->hte", query_heads, prior_state, precision=PRECISE
    )
    attended = inside_part + outside_part
    square_mean = jnp.mean(attended * attended, axis=2, keepdims=True)
    heads_normed = (
        attended * lax.rsqrt(square_mean + 1e-05) * attn_gain.reshape(heads_here, 1, head_size)
    )
    heads_normed = (
        heads_normed.astype(jnp.bfloat16)
        .transpose(1, 0, 2)
        .reshape(token_count, heads_here * head_size)
    )
    ctx_size = lax.axis_size("ctx")
    head_count = lax.axis_size("head")
    weight_blocks = lax.all_gather(out_weight, "ctx")
    model_width = residual.shape[1]
    experts_total = router.shape[1]
    capacity = 2 * token_count * TOP // experts_total
    slice_width = model_width // head_count
    slice_start = lax.axis_index("head") * slice_width
    partial_out = jnp.einsum(
        "tk,ckd->tcd", heads_normed, weight_blocks, preferred_element_type=jnp.float32
    ).reshape(token_count, head_count, slice_width)
    pieces = lax.all_to_all(
        partial_out.astype(jnp.bfloat16).transpose(1, 0, 2),
        "head",
        split_axis=0,
        concat_axis=0,
        tiled=True,
    )
    projected = jnp.sum(pieces.astype(jnp.float32), axis=0)
    own_residual = lax.dynamic_slice_in_dim(residual, slice_start, slice_width, 1)
    mixed_slice = (own_residual.astype(jnp.float32) + projected).astype(jnp.bfloat16)
    mixed_all = lax.all_to_all(
        jnp.broadcast_to(mixed_slice[None], (head_count,) + mixed_slice.shape),
        "head",
        split_axis=0,
        concat_axis=0,
        tiled=True,
    )
    mixed_rows = mixed_all.transpose(1, 0, 2).reshape(token_count, model_width)
    mixed_wide = mixed_rows.astype(jnp.float32)
    inv_rms = lax.rsqrt(jnp.mean(mixed_wide * mixed_wide, axis=1, keepdims=True) + 1e-06)
    scaled = mixed_wide * moe_gain[None, :]
    moe_in = (scaled * inv_rms).astype(jnp.bfloat16)
    logits = inv_rms * jnp.dot(scaled, router, precision=PRECISE)
    base_slice = lax.dynamic_slice_in_dim(mixed_wide, slice_start, slice_width, 1)
    gate_weights, slot_index = route_tokens(logits, expert_ids, experts_total)
    target = (expert_ids * capacity + slot_index).reshape(-1)
    width_here = moe_in.shape[1]
    source = jnp.repeat(moe_in, TOP, axis=0)
    packed = jnp.zeros((experts_total * capacity, width_here), jnp.bfloat16).at[target].set(source)
    arrived = lax.all_to_all(
        packed.reshape(experts_total, capacity, width_here),
        "ctx",
        split_axis=0,
        concat_axis=0,
        tiled=True,
    )
    flat_rows = arrived.reshape(-1, model_width)
    gate_part = jnp.dot(flat_rows, w_gate[0], preferred_element_type=jnp.float32)
    up_part = jnp.dot(flat_rows, w_up[0], preferred_element_type=jnp.float32)
    hidden = (jax.nn.silu(gate_part) * up_part).astype(jnp.bfloat16)
    partial_down = jnp.dot(hidden, w_down[0], preferred_element_type=jnp.float32)
    summed = lax.psum_scatter(
        partial_down.astype(jnp.bfloat16), "head", scatter_dimension=1, tiled=True
    )
    returned = lax.all_to_all(
        summed.reshape(experts_total, capacity, slice_width),
        "ctx",
        split_axis=0,
        concat_axis=0,
        tiled=True,
    )
    lookup = returned.reshape(experts_total * capacity, slice_width)
    picked = lookup[target].reshape(token_count, TOP, slice_width).astype(jnp.float32)
    final_out = (
        base_slice + gate_weights[:, 0:1] * picked[:, 0] + gate_weights[:, 1:2] * picked[:, 1]
    )
    return final_out.astype(jnp.bfloat16)


def solution(mesh):
    in_specs = (
        P("ctx", "head"),
        P("ctx", "head"),
        P("ctx", "head"),
        P("head", "ctx"),
        P("ctx", None),
        P("head", "ctx"),
        P("head"),
        P(),
        P(),
        P("ctx", None, "head"),
        P("ctx", None, "head"),
        P("ctx", "head", None),
        P("ctx", None),
    )
    out_specs = P("ctx", "head")
    return jax.shard_map(body, mesh=mesh, in_specs=in_specs, out_specs=out_specs, check_vma=False)
```

```python
import jax
import jax.numpy as jnp
from jax import lax
from jax.sharding import PartitionSpec as P

TOP = 2


PRECISE = lax.Precision.HIGHEST


def prior_states(final_log, local_state, axis):
    peers = lax.axis_size(axis)
    heads_here, head_size = local_state.shape[0], local_state.shape[2]
    totals = jnp.broadcast_to(final_log[:, None, None], (heads_here, 8, head_size))
    packed = jnp.concatenate([local_state, totals], axis=1)
    row = lax.broadcasted_iota(jnp.int32, packed.shape, 1)

    def combine(earlier, later):
        scale = jnp.exp(later[:, head_size : head_size + 1, 0:1])
        return later + jnp.where(row < head_size, scale, 1.0) * earlier

    def shifted(value, distance):
        pairs = [(k, k + distance) for k in range(peers - distance)]
        return lax.ppermute(value, axis, pairs)

    radix = 4
    before = shifted(packed, 1)
    for distance in range(2, radix + 1):
        before = combine(shifted(packed, distance), before)
    covered = radix
    while covered < peers:
        reached = before
        for times in range(1, radix):
            if covered * times < peers:
                reached = combine(shifted(before, covered * times), reached)
        before = reached
        covered *= radix
    return before[:, :head_size]


def local_attention(query_block, key_block, value_block, decay_block):
    running = jnp.cumsum(decay_block, axis=1)
    length_here = decay_block.shape[1]
    row_index = lax.broadcasted_iota(jnp.int32, (length_here, length_here), 0)
    col_index = lax.broadcasted_iota(jnp.int32, (length_here, length_here), 1)
    causal = (col_index <= row_index)[None]
    spread = jnp.where(causal, running[:, :, None] - running[:, None, :], 0.0)
    decay_weights = jnp.where(causal, jnp.exp(spread), 0.0)
    scores = jnp.einsum("htd,hsd->hts", query_block, key_block, precision=PRECISE) * decay_weights
    inside_part = jnp.einsum("hts,hse->hte", scores, value_block, precision=PRECISE)
    final_log = running[:, -1]
    tail_decay = jnp.exp(final_log[:, None] - running)
    local_state = jnp.einsum(
        "hsd,hse->hde", key_block * tail_decay[:, :, None], value_block, precision=PRECISE
    )
    return (inside_part, running, local_state, final_log)


def route_tokens(logits, expert_ids, experts_total):
    onehot = expert_ids[:, :, None] == lax.broadcasted_iota(jnp.int32, (1, 1, experts_total), 2)
    chosen = jnp.sum(jnp.where(onehot, logits[:, None, :], 0.0), axis=2)
    leading = jax.nn.sigmoid(chosen[:, 0] - chosen[:, 1])
    gate_weights = jnp.stack([leading, 1.0 - leading], axis=1)
    marked = onehot.reshape(-1, experts_total).astype(jnp.int32)
    earlier = jnp.cumsum(marked, axis=0) - marked
    slot_index = jnp.sum(earlier * marked, axis=1).reshape(expert_ids.shape)
    return (gate_weights, slot_index)


def body(
    query_vectors,
    key_vectors,
    value_vectors,
    log_decay,
    residual,
    out_weight,
    attn_gain,
    moe_gain,
    router,
    w_gate,
    w_up,
    w_down,
    expert_ids,
):
    token_count = query_vectors.shape[0]
    heads_here = log_decay.shape[0]
    head_size = query_vectors.shape[1] // heads_here

    def split_heads(matrix_in):
        return (
            matrix_in.astype(jnp.float32)
            .reshape(token_count, heads_here, head_size)
            .transpose(1, 0, 2)
        )

    query_heads = split_heads(query_vectors)
    inside_part, running, local_state, final_log = local_attention(
        query_heads, split_heads(key_vectors), split_heads(value_vectors), log_decay
    )
    prior_state = prior_states(final_log, local_state, "ctx")
    outside_part = jnp.exp(running)[:, :, None] * jnp.einsum(
        "htd,hde->hte", query_heads, prior_state, precision=PRECISE
    )
    attended = inside_part + outside_part
    square_mean = jnp.mean(attended * attended, axis=2, keepdims=True)
    heads_normed = (
        attended * lax.rsqrt(square_mean + 1e-05) * attn_gain.reshape(heads_here, 1, head_size)
    )
    heads_normed = (
        heads_normed.astype(jnp.bfloat16)
        .transpose(1, 0, 2)
        .reshape(token_count, heads_here * head_size)
    )
    ctx_size = lax.axis_size("ctx")
    head_count = lax.axis_size("head")
    weight_blocks = lax.all_gather(out_weight, "ctx")
    model_width = residual.shape[1]
    experts_total = router.shape[1]
    capacity = 2 * token_count * TOP // experts_total
    slice_width = model_width // head_count
    slice_start = lax.axis_index("head") * slice_width
    partial_out = jnp.einsum(
        "tk,ckd->tcd", heads_normed, weight_blocks, preferred_element_type=jnp.float32
    ).reshape(token_count, model_width)
    projected = lax.psum_scatter(
        partial_out.astype(jnp.bfloat16), "head", scatter_dimension=1, tiled=True
    ).astype(jnp.float32)
    own_residual = lax.dynamic_slice_in_dim(residual, slice_start, slice_width, 1)
    mixed_slice = (own_residual.astype(jnp.float32) + projected).astype(jnp.bfloat16)
    mixed_all = lax.all_to_all(
        jnp.broadcast_to(mixed_slice[None], (head_count,) + mixed_slice.shape),
        "head",
        split_axis=0,
        concat_axis=0,
        tiled=True,
    )
    mixed_rows = mixed_all.transpose(1, 0, 2).reshape(token_count, model_width)
    mixed_wide = mixed_rows.astype(jnp.float32)
    inv_rms = lax.rsqrt(jnp.mean(mixed_wide * mixed_wide, axis=1, keepdims=True) + 1e-06)
    scaled = mixed_wide * moe_gain[None, :]
    moe_in = (scaled * inv_rms).astype(jnp.bfloat16)
    logits = inv_rms * jnp.dot(scaled, router, precision=PRECISE)
    base_slice = lax.dynamic_slice_in_dim(mixed_wide, slice_start, slice_width, 1)
    gate_weights, slot_index = route_tokens(logits, expert_ids, experts_total)
    target = (expert_ids * capacity + slot_index).reshape(-1)
    width_here = moe_in.shape[1]
    source = jnp.repeat(moe_in, TOP, axis=0)
    packed = jnp.zeros((experts_total * capacity, width_here), jnp.bfloat16).at[target].set(source)
    arrived = lax.all_to_all(
        packed.reshape(experts_total, capacity, width_here),
        "ctx",
        split_axis=0,
        concat_axis=0,
        tiled=True,
    )
    flat_rows = arrived.reshape(-1, model_width)
    gate_part = jnp.dot(flat_rows, w_gate[0], preferred_element_type=jnp.float32)
    up_part = jnp.dot(flat_rows, w_up[0], preferred_element_type=jnp.float32)
    hidden = (jax.nn.silu(gate_part) * up_part).astype(jnp.bfloat16)
    partial_down = jnp.dot(hidden, w_down[0], preferred_element_type=jnp.float32)
    summed = lax.psum_scatter(
        partial_down.astype(jnp.bfloat16), "head", scatter_dimension=1, tiled=True
    )
    returned = lax.all_to_all(
        summed.reshape(experts_total, capacity, slice_width),
        "ctx",
        split_axis=0,
        concat_axis=0,
        tiled=True,
    )
    lookup = returned.reshape(experts_total * capacity, slice_width)
    picked = lookup[target].reshape(token_count, TOP, slice_width).astype(jnp.float32)
    final_out = (
        base_slice + gate_weights[:, 0:1] * picked[:, 0] + gate_weights[:, 1:2] * picked[:, 1]
    )
    return final_out.astype(jnp.bfloat16)


def solution(mesh):
    in_specs = (
        P("ctx", "head"),
        P("ctx", "head"),
        P("ctx", "head"),
        P("head", "ctx"),
        P("ctx", None),
        P("head", "ctx"),
        P("head"),
        P(),
        P(),
        P("ctx", None, "head"),
        P("ctx", None, "head"),
        P("ctx", "head", None),
        P("ctx", None),
    )
    out_specs = P("ctx", "head")
    return jax.shard_map(body, mesh=mesh, in_specs=in_specs, out_specs=out_specs, check_vma=False)
```

```python
import jax
import jax.numpy as jnp
from jax import lax
from jax.sharding import PartitionSpec as P

TOP = 2


PRECISE = lax.Precision.HIGHEST


def prior_states(final_log, local_state, axis):
    peers = lax.axis_size(axis)
    heads_here, head_size = local_state.shape[0], local_state.shape[2]
    totals = jnp.broadcast_to(final_log[:, None, None], (heads_here, 8, head_size))
    packed = jnp.concatenate([local_state, totals], axis=1)
    row = lax.broadcasted_iota(jnp.int32, packed.shape, 1)

    def combine(earlier, later):
        scale = jnp.exp(later[:, head_size : head_size + 1, 0:1])
        return later + jnp.where(row < head_size, scale, 1.0) * earlier

    def shifted(value, distance):
        pairs = [(k, k + distance) for k in range(peers - distance)]
        return lax.ppermute(value, axis, pairs)

    before = combine(shifted(packed, 2), shifted(packed, 1))
    distance = 2
    while distance < peers:
        before = combine(shifted(before, distance), before)
        distance *= 2
    return before[:, :head_size]


def local_attention(query_block, key_block, value_block, decay_block):
    running = jnp.cumsum(decay_block, axis=1)
    length_here = decay_block.shape[1]
    row_index = lax.broadcasted_iota(jnp.int32, (length_here, length_here), 0)
    col_index = lax.broadcasted_iota(jnp.int32, (length_here, length_here), 1)
    causal = (col_index <= row_index)[None]
    spread = jnp.where(causal, running[:, :, None] - running[:, None, :], 0.0)
    decay_weights = jnp.where(causal, jnp.exp(spread), 0.0)
    scores = jnp.einsum("htd,hsd->hts", query_block, key_block, precision=PRECISE) * decay_weights
    inside_part = jnp.einsum("hts,hse->hte", scores, value_block, precision=PRECISE)
    final_log = running[:, -1]
    tail_decay = jnp.exp(final_log[:, None] - running)
    local_state = jnp.einsum(
        "hsd,hse->hde", key_block * tail_decay[:, :, None], value_block, precision=PRECISE
    )
    return (inside_part, running, local_state, final_log)


def route_tokens(logits, expert_ids, experts_total):
    onehot = expert_ids[:, :, None] == lax.broadcasted_iota(jnp.int32, (1, 1, experts_total), 2)
    chosen = jnp.sum(jnp.where(onehot, logits[:, None, :], 0.0), axis=2)
    leading = jax.nn.sigmoid(chosen[:, 0] - chosen[:, 1])
    gate_weights = jnp.stack([leading, 1.0 - leading], axis=1)
    marked = onehot.reshape(-1, experts_total).astype(jnp.int32)
    earlier = jnp.cumsum(marked, axis=0) - marked
    slot_index = jnp.sum(earlier * marked, axis=1).reshape(expert_ids.shape)
    return (gate_weights, slot_index)


def body(
    query_vectors,
    key_vectors,
    value_vectors,
    log_decay,
    residual,
    out_weight,
    attn_gain,
    moe_gain,
    router,
    w_gate,
    w_up,
    w_down,
    expert_ids,
):
    token_count = query_vectors.shape[0]
    heads_here = log_decay.shape[0]
    head_size = query_vectors.shape[1] // heads_here

    def split_heads(matrix_in):
        return (
            matrix_in.astype(jnp.float32)
            .reshape(token_count, heads_here, head_size)
            .transpose(1, 0, 2)
        )

    query_heads = split_heads(query_vectors)
    inside_part, running, local_state, final_log = local_attention(
        query_heads, split_heads(key_vectors), split_heads(value_vectors), log_decay
    )
    prior_state = prior_states(final_log, local_state, "ctx")
    outside_part = jnp.exp(running)[:, :, None] * jnp.einsum(
        "htd,hde->hte", query_heads, prior_state, precision=PRECISE
    )
    attended = inside_part + outside_part
    square_mean = jnp.mean(attended * attended, axis=2, keepdims=True)
    heads_normed = (
        attended * lax.rsqrt(square_mean + 1e-05) * attn_gain.reshape(heads_here, 1, head_size)
    )
    heads_normed = (
        heads_normed.astype(jnp.bfloat16)
        .transpose(1, 0, 2)
        .reshape(token_count, heads_here * head_size)
    )
    ctx_size = lax.axis_size("ctx")
    head_count = lax.axis_size("head")
    weight_blocks = lax.all_gather(out_weight, "ctx")
    model_width = residual.shape[1]
    experts_total = router.shape[1]
    capacity = 2 * token_count * TOP // experts_total
    slice_width = model_width // head_count
    slice_start = lax.axis_index("head") * slice_width
    partial_out = jnp.einsum(
        "tk,ckd->tcd", heads_normed, weight_blocks, preferred_element_type=jnp.float32
    ).reshape(token_count, head_count, slice_width)
    pieces = lax.all_to_all(
        partial_out.astype(jnp.bfloat16).transpose(1, 0, 2),
        "head",
        split_axis=0,
        concat_axis=0,
        tiled=True,
    )
    projected = jnp.sum(pieces.astype(jnp.float32), axis=0)
    own_residual = lax.dynamic_slice_in_dim(residual, slice_start, slice_width, 1)
    mixed_slice = (own_residual.astype(jnp.float32) + projected).astype(jnp.bfloat16)
    mixed_all = lax.all_to_all(
        jnp.broadcast_to(mixed_slice[None], (head_count,) + mixed_slice.shape),
        "head",
        split_axis=0,
        concat_axis=0,
        tiled=True,
    )
    mixed_rows = mixed_all.transpose(1, 0, 2).reshape(token_count, model_width)
    mixed_wide = mixed_rows.astype(jnp.float32)
    inv_rms = lax.rsqrt(jnp.mean(mixed_wide * mixed_wide, axis=1, keepdims=True) + 1e-06)
    scaled = mixed_wide * moe_gain[None, :]
    moe_in = (scaled * inv_rms).astype(jnp.bfloat16)
    logits = inv_rms * jnp.dot(scaled, router, precision=PRECISE)
    base_slice = lax.dynamic_slice_in_dim(mixed_wide, slice_start, slice_width, 1)
    gate_weights, slot_index = route_tokens(logits, expert_ids, experts_total)
    target = (expert_ids * capacity + slot_index).reshape(-1)
    width_here = moe_in.shape[1]
    slots = lax.broadcasted_iota(jnp.int32, (experts_total * capacity, token_count, TOP), 0)
    chosen = jnp.any(slots == target.reshape(token_count, TOP)[None], axis=2)
    packed = jnp.dot(
        chosen.astype(jnp.bfloat16), moe_in, preferred_element_type=jnp.float32
    ).astype(jnp.bfloat16)
    arrived = lax.all_to_all(
        packed.reshape(experts_total, capacity, width_here),
        "ctx",
        split_axis=0,
        concat_axis=0,
        tiled=True,
    )
    flat_rows = arrived.reshape(-1, model_width)
    gate_part = jnp.dot(flat_rows, w_gate[0], preferred_element_type=jnp.float32)
    up_part = jnp.dot(flat_rows, w_up[0], preferred_element_type=jnp.float32)
    hidden = (jax.nn.silu(gate_part) * up_part).astype(jnp.bfloat16)
    partial_down = jnp.dot(hidden, w_down[0], preferred_element_type=jnp.float32)
    summed = lax.psum_scatter(
        partial_down.astype(jnp.bfloat16), "head", scatter_dimension=1, tiled=True
    )
    returned = lax.all_to_all(
        summed.reshape(experts_total, capacity, slice_width),
        "ctx",
        split_axis=0,
        concat_axis=0,
        tiled=True,
    )
    lookup = returned.reshape(experts_total * capacity, slice_width)
    columns = lax.broadcasted_iota(jnp.int32, (token_count, experts_total * capacity), 1)
    ranked = target.reshape(token_count, TOP)
    picked = [
        jnp.dot(
            (columns == ranked[:, k : k + 1]).astype(jnp.bfloat16),
            lookup,
            preferred_element_type=jnp.float32,
        )
        for k in range(TOP)
    ]
    final_out = base_slice + gate_weights[:, 0:1] * picked[0] + gate_weights[:, 1:2] * picked[1]
    return final_out.astype(jnp.bfloat16)


def solution(mesh):
    in_specs = (
        P("ctx", "head"),
        P("ctx", "head"),
        P("ctx", "head"),
        P("head", "ctx"),
        P("ctx", None),
        P("head", "ctx"),
        P("head"),
        P(),
        P(),
        P("ctx", None, "head"),
        P("ctx", None, "head"),
        P("ctx", "head", None),
        P("ctx", None),
    )
    out_specs = P("ctx", "head")
    return jax.shard_map(body, mesh=mesh, in_specs=in_specs, out_specs=out_specs, check_vma=False)
```

```python
import jax
import jax.numpy as jnp
from jax import lax
from jax.sharding import PartitionSpec as P

TOP = 2


PRECISE = lax.Precision.HIGHEST


def prior_states(final_log, local_state, axis):
    peers = lax.axis_size(axis)
    heads_here, head_size = local_state.shape[0], local_state.shape[2]

    def pack(value):
        state, total = value
        high = total.astype(jnp.bfloat16)
        rest = total - high.astype(jnp.float32)
        middle = rest.astype(jnp.bfloat16)
        low = (rest - middle.astype(jnp.float32)).astype(jnp.bfloat16)
        extra = jnp.zeros((heads_here, 16, head_size), jnp.bfloat16)
        extra = extra.at[:, 0:3, 0].set(jnp.stack([high, middle, low], axis=1))
        return jnp.concatenate([state.astype(jnp.bfloat16), extra], axis=1)

    def unpack(packed):
        state = packed[:, :head_size].astype(jnp.float32)
        total = jnp.sum(packed[:, head_size : head_size + 3, 0].astype(jnp.float32), axis=1)
        return (state, total)

    def combine(earlier, later):
        return (
            jnp.exp(later[1])[:, None, None] * earlier[0] + later[0],
            earlier[1] + later[1],
        )

    def shifted(value, distance):
        pairs = [(k, k + distance) for k in range(peers - distance)]
        return unpack(lax.ppermute(pack(value), axis, pairs))

    own = (local_state, final_log)
    before = combine(shifted(own, 2), shifted(own, 1))
    distance = 2
    while distance < peers:
        before = combine(shifted(before, distance), before)
        distance *= 2
    return before[0]


def local_attention(query_block, key_block, value_block, decay_block):
    running = jnp.cumsum(decay_block, axis=1)
    length_here = decay_block.shape[1]
    row_index = lax.broadcasted_iota(jnp.int32, (length_here, length_here), 0)
    col_index = lax.broadcasted_iota(jnp.int32, (length_here, length_here), 1)
    causal = (col_index <= row_index)[None]
    spread = jnp.where(causal, running[:, :, None] - running[:, None, :], 0.0)
    decay_weights = jnp.where(causal, jnp.exp(spread), 0.0)
    scores = jnp.einsum("htd,hsd->hts", query_block, key_block, precision=PRECISE) * decay_weights
    inside_part = jnp.einsum("hts,hse->hte", scores, value_block, precision=PRECISE)
    final_log = running[:, -1]
    tail_decay = jnp.exp(final_log[:, None] - running)
    local_state = jnp.einsum(
        "hsd,hse->hde", key_block * tail_decay[:, :, None], value_block, precision=PRECISE
    )
    return (inside_part, running, local_state, final_log)


def route_tokens(logits, expert_ids, experts_total):
    onehot = expert_ids[:, :, None] == lax.broadcasted_iota(jnp.int32, (1, 1, experts_total), 2)
    chosen = jnp.sum(jnp.where(onehot, logits[:, None, :], 0.0), axis=2)
    leading = jax.nn.sigmoid(chosen[:, 0] - chosen[:, 1])
    gate_weights = jnp.stack([leading, 1.0 - leading], axis=1)
    marked = onehot.reshape(-1, experts_total).astype(jnp.int32)
    earlier = jnp.cumsum(marked, axis=0) - marked
    slot_index = jnp.sum(earlier * marked, axis=1).reshape(expert_ids.shape)
    return (gate_weights, slot_index)


def body(
    query_vectors,
    key_vectors,
    value_vectors,
    log_decay,
    residual,
    out_weight,
    attn_gain,
    moe_gain,
    router,
    w_gate,
    w_up,
    w_down,
    expert_ids,
):
    token_count = query_vectors.shape[0]
    heads_here = log_decay.shape[0]
    head_size = query_vectors.shape[1] // heads_here

    def split_heads(matrix_in):
        return (
            matrix_in.astype(jnp.float32)
            .reshape(token_count, heads_here, head_size)
            .transpose(1, 0, 2)
        )

    query_heads = split_heads(query_vectors)
    inside_part, running, local_state, final_log = local_attention(
        query_heads, split_heads(key_vectors), split_heads(value_vectors), log_decay
    )
    prior_state = prior_states(final_log, local_state, "ctx")
    outside_part = jnp.exp(running)[:, :, None] * jnp.einsum(
        "htd,hde->hte", query_heads, prior_state, precision=PRECISE
    )
    attended = inside_part + outside_part
    square_mean = jnp.mean(attended * attended, axis=2, keepdims=True)
    heads_normed = (
        attended * lax.rsqrt(square_mean + 1e-05) * attn_gain.reshape(heads_here, 1, head_size)
    )
    heads_normed = (
        heads_normed.astype(jnp.bfloat16)
        .transpose(1, 0, 2)
        .reshape(token_count, heads_here * head_size)
    )
    ctx_size = lax.axis_size("ctx")
    head_count = lax.axis_size("head")
    weight_blocks = lax.all_gather(out_weight, "ctx")
    model_width = residual.shape[1]
    experts_total = router.shape[1]
    capacity = 2 * token_count * TOP // experts_total
    slice_width = model_width // head_count
    slice_start = lax.axis_index("head") * slice_width
    partial_out = jnp.einsum(
        "tk,ckd->tcd", heads_normed, weight_blocks, preferred_element_type=jnp.float32
    ).reshape(token_count, head_count, slice_width)
    pieces = lax.all_to_all(
        partial_out.astype(jnp.bfloat16).transpose(1, 0, 2),
        "head",
        split_axis=0,
        concat_axis=0,
        tiled=True,
    )
    projected = jnp.sum(pieces.astype(jnp.float32), axis=0)
    own_residual = lax.dynamic_slice_in_dim(residual, slice_start, slice_width, 1)
    mixed_slice = (own_residual.astype(jnp.float32) + projected).astype(jnp.bfloat16)
    mixed_all = lax.all_to_all(
        jnp.broadcast_to(mixed_slice[None], (head_count,) + mixed_slice.shape),
        "head",
        split_axis=0,
        concat_axis=0,
        tiled=True,
    )
    mixed_rows = mixed_all.transpose(1, 0, 2).reshape(token_count, model_width)
    mixed_wide = mixed_rows.astype(jnp.float32)
    inv_rms = lax.rsqrt(jnp.mean(mixed_wide * mixed_wide, axis=1, keepdims=True) + 1e-06)
    scaled = mixed_wide * moe_gain[None, :]
    moe_in = (scaled * inv_rms).astype(jnp.bfloat16)
    logits = inv_rms * jnp.dot(scaled, router, precision=PRECISE)
    base_slice = lax.dynamic_slice_in_dim(mixed_wide, slice_start, slice_width, 1)
    gate_weights, slot_index = route_tokens(logits, expert_ids, experts_total)
    target = (expert_ids * capacity + slot_index).reshape(-1)
    width_here = moe_in.shape[1]
    slots = lax.broadcasted_iota(jnp.int32, (experts_total * capacity, token_count, TOP), 0)
    chosen = jnp.any(slots == target.reshape(token_count, TOP)[None], axis=2)
    packed = jnp.dot(
        chosen.astype(jnp.bfloat16), moe_in, preferred_element_type=jnp.float32
    ).astype(jnp.bfloat16)
    arrived = lax.all_to_all(
        packed.reshape(experts_total, capacity, width_here),
        "ctx",
        split_axis=0,
        concat_axis=0,
        tiled=True,
    )
    flat_rows = arrived.reshape(-1, model_width)
    gate_part = jnp.dot(flat_rows, w_gate[0], preferred_element_type=jnp.float32)
    up_part = jnp.dot(flat_rows, w_up[0], preferred_element_type=jnp.float32)
    hidden = (jax.nn.silu(gate_part) * up_part).astype(jnp.bfloat16)
    partial_down = jnp.dot(hidden, w_down[0], preferred_element_type=jnp.float32)
    summed = lax.psum_scatter(
        partial_down.astype(jnp.bfloat16), "head", scatter_dimension=1, tiled=True
    )
    returned = lax.all_to_all(
        summed.reshape(experts_total, capacity, slice_width),
        "ctx",
        split_axis=0,
        concat_axis=0,
        tiled=True,
    )
    lookup = returned.reshape(experts_total * capacity, slice_width)
    columns = lax.broadcasted_iota(jnp.int32, (token_count, experts_total * capacity), 1)
    ranked = target.reshape(token_count, TOP)
    picked = [
        jnp.dot(
            (columns == ranked[:, k : k + 1]).astype(jnp.bfloat16),
            lookup,
            preferred_element_type=jnp.float32,
        )
        for k in range(TOP)
    ]
    final_out = base_slice + gate_weights[:, 0:1] * picked[0] + gate_weights[:, 1:2] * picked[1]
    return final_out.astype(jnp.bfloat16)


def solution(mesh):
    in_specs = (
        P("ctx", "head"),
        P("ctx", "head"),
        P("ctx", "head"),
        P("head", "ctx"),
        P("ctx", None),
        P("head", "ctx"),
        P("head"),
        P(),
        P(),
        P("ctx", None, "head"),
        P("ctx", None, "head"),
        P("ctx", "head", None),
        P("ctx", None),
    )
    out_specs = P("ctx", "head")
    return jax.shard_map(body, mesh=mesh, in_specs=in_specs, out_specs=out_specs, check_vma=False)
```

```python
import jax
import jax.numpy as jnp
from jax import lax
from jax.sharding import PartitionSpec as P

TOP = 2


PRECISE = lax.Precision.HIGHEST


def prior_states(final_log, local_state, axis):
    peers = lax.axis_size(axis)
    heads_here, head_size = local_state.shape[0], local_state.shape[2]

    def pack(value):
        state, total = value
        high = total.astype(jnp.bfloat16)
        rest = total - high.astype(jnp.float32)
        middle = rest.astype(jnp.bfloat16)
        low = (rest - middle.astype(jnp.float32)).astype(jnp.bfloat16)
        extra = jnp.zeros((heads_here, 16, head_size), jnp.bfloat16)
        extra = extra.at[:, 0:3, 0].set(jnp.stack([high, middle, low], axis=1))
        return jnp.concatenate([state.astype(jnp.bfloat16), extra], axis=1)

    def unpack(packed):
        state = packed[:, :head_size].astype(jnp.float32)
        total = jnp.sum(packed[:, head_size : head_size + 3, 0].astype(jnp.float32), axis=1)
        return (state, total)

    def combine(earlier, later):
        return (
            jnp.exp(later[1])[:, None, None] * earlier[0] + later[0],
            earlier[1] + later[1],
        )

    def shifted(value, distance):
        pairs = [(k, k + distance) for k in range(peers - distance)]
        return unpack(lax.ppermute(pack(value), axis, pairs))

    own = (local_state, final_log)
    before = combine(shifted(own, 2), shifted(own, 1))
    distance = 2
    while distance < peers:
        before = combine(shifted(before, distance), before)
        distance *= 2
    return before[0]


def local_attention(query_block, key_block, value_block, decay_block):
    running = jnp.cumsum(decay_block, axis=1)
    length_here = decay_block.shape[1]
    row_index = lax.broadcasted_iota(jnp.int32, (length_here, length_here), 0)
    col_index = lax.broadcasted_iota(jnp.int32, (length_here, length_here), 1)
    causal = (col_index <= row_index)[None]
    spread = jnp.where(causal, running[:, :, None] - running[:, None, :], 0.0)
    decay_weights = jnp.where(causal, jnp.exp(spread), 0.0)
    scores = jnp.einsum("htd,hsd->hts", query_block, key_block, precision=PRECISE) * decay_weights
    inside_part = jnp.einsum("hts,hse->hte", scores, value_block, precision=PRECISE)
    final_log = running[:, -1]
    tail_decay = jnp.exp(final_log[:, None] - running)
    local_state = jnp.einsum(
        "hsd,hse->hde", key_block * tail_decay[:, :, None], value_block, precision=PRECISE
    )
    return (inside_part, running, local_state, final_log)


def route_tokens(logits, expert_ids, experts_total):
    onehot = expert_ids[:, :, None] == lax.broadcasted_iota(jnp.int32, (1, 1, experts_total), 2)
    chosen = jnp.sum(jnp.where(onehot, logits[:, None, :], 0.0), axis=2)
    leading = jax.nn.sigmoid(chosen[:, 0] - chosen[:, 1])
    gate_weights = jnp.stack([leading, 1.0 - leading], axis=1)
    marked = onehot.reshape(-1, experts_total).astype(jnp.int32)
    earlier = jnp.cumsum(marked, axis=0) - marked
    slot_index = jnp.sum(earlier * marked, axis=1).reshape(expert_ids.shape)
    return (gate_weights, slot_index)


def body(
    query_vectors,
    key_vectors,
    value_vectors,
    log_decay,
    residual,
    out_weight,
    attn_gain,
    moe_gain,
    router,
    w_gate,
    w_up,
    w_down,
    expert_ids,
):
    token_count = query_vectors.shape[0]
    heads_here = log_decay.shape[0]
    head_size = query_vectors.shape[1] // heads_here

    def split_heads(matrix_in):
        return (
            matrix_in.astype(jnp.float32)
            .reshape(token_count, heads_here, head_size)
            .transpose(1, 0, 2)
        )

    query_heads = split_heads(query_vectors)
    inside_part, running, local_state, final_log = local_attention(
        query_heads, split_heads(key_vectors), split_heads(value_vectors), log_decay
    )
    prior_state = prior_states(final_log, local_state, "ctx")
    outside_part = jnp.exp(running)[:, :, None] * jnp.einsum(
        "htd,hde->hte", query_heads, prior_state, precision=PRECISE
    )
    attended = inside_part + outside_part
    square_mean = jnp.mean(attended * attended, axis=2, keepdims=True)
    heads_normed = (
        attended * lax.rsqrt(square_mean + 1e-05) * attn_gain.reshape(heads_here, 1, head_size)
    )
    heads_normed = (
        heads_normed.astype(jnp.bfloat16)
        .transpose(1, 0, 2)
        .reshape(token_count, heads_here * head_size)
    )
    ctx_size = lax.axis_size("ctx")
    head_count = lax.axis_size("head")
    weight_blocks = lax.all_gather(out_weight, "ctx")
    model_width = residual.shape[1]
    experts_total = router.shape[1]
    capacity = 2 * token_count * TOP // experts_total
    slice_width = model_width // head_count
    slice_start = lax.axis_index("head") * slice_width
    partial_out = jnp.einsum(
        "tk,ckd->tcd", heads_normed, weight_blocks, preferred_element_type=jnp.float32
    ).reshape(token_count, head_count, slice_width)
    pieces = lax.all_to_all(
        partial_out.astype(jnp.bfloat16).transpose(1, 0, 2),
        "head",
        split_axis=0,
        concat_axis=0,
        tiled=True,
    )
    projected = jnp.sum(pieces.astype(jnp.float32), axis=0)
    own_residual = lax.dynamic_slice_in_dim(residual, slice_start, slice_width, 1)
    mixed_slice = (own_residual.astype(jnp.float32) + projected).astype(jnp.bfloat16)
    mixed_part = mixed_slice.astype(jnp.float32)
    gain_slice = lax.dynamic_slice_in_dim(moe_gain, slice_start, slice_width, 0)
    router_slice = lax.dynamic_slice_in_dim(router, slice_start, slice_width, 0)
    partial_logits = jnp.dot(mixed_part * gain_slice[None, :], router_slice, precision=PRECISE)
    partial_squares = jnp.sum(mixed_part * mixed_part, axis=1, keepdims=True)
    reduced = lax.psum(jnp.concatenate([partial_logits, partial_squares], axis=1), "head")
    inv_rms = lax.rsqrt(reduced[:, experts_total:] / model_width + 1e-06)
    logits = inv_rms * reduced[:, :experts_total]
    base_slice = mixed_part
    gate_weights, slot_index = route_tokens(logits, expert_ids, experts_total)
    target = (expert_ids * capacity + slot_index).reshape(-1)
    slots = lax.broadcasted_iota(jnp.int32, (experts_total * capacity, token_count, TOP), 0)
    chosen = jnp.any(slots == target.reshape(token_count, TOP)[None], axis=2)
    packed = jnp.dot(
        chosen.astype(jnp.bfloat16), mixed_slice, preferred_element_type=jnp.float32
    ).astype(jnp.bfloat16)
    spread = jnp.broadcast_to(
        packed.reshape(experts_total, 1, capacity, slice_width),
        (experts_total, head_count, capacity, slice_width),
    )
    arrived = lax.all_to_all(
        spread.reshape(-1, slice_width), ("ctx", "head"), split_axis=0, concat_axis=0, tiled=True
    ).reshape(ctx_size, head_count, capacity, slice_width)
    rows = arrived.astype(jnp.float32)
    inv_rows = lax.rsqrt(jnp.sum(rows * rows, axis=(1, 3)) / model_width + 1e-06)
    moe_rows = (
        rows * moe_gain.reshape(1, head_count, 1, slice_width) * inv_rows[:, None, :, None]
    ).astype(jnp.bfloat16)
    hidden_width = w_gate.shape[2]
    gate_part = jnp.einsum(
        "chsj,hjf->csf",
        moe_rows,
        w_gate[0].reshape(head_count, slice_width, hidden_width),
        preferred_element_type=jnp.float32,
    )
    up_part = jnp.einsum(
        "chsj,hjf->csf",
        moe_rows,
        w_up[0].reshape(head_count, slice_width, hidden_width),
        preferred_element_type=jnp.float32,
    )
    hidden = (jax.nn.silu(gate_part) * up_part).astype(jnp.bfloat16)
    partial_down = jnp.einsum(
        "csf,fd->csd", hidden, w_down[0], preferred_element_type=jnp.float32
    ).reshape(ctx_size * capacity, model_width)
    summed = lax.psum_scatter(
        partial_down.astype(jnp.bfloat16), "head", scatter_dimension=1, tiled=True
    )
    returned = lax.all_to_all(
        summed.reshape(experts_total, capacity, slice_width),
        "ctx",
        split_axis=0,
        concat_axis=0,
        tiled=True,
    )
    lookup = returned.reshape(experts_total * capacity, slice_width)
    columns = lax.broadcasted_iota(jnp.int32, (token_count, experts_total * capacity), 1)
    ranked = target.reshape(token_count, TOP)
    picked = [
        jnp.dot(
            (columns == ranked[:, k : k + 1]).astype(jnp.bfloat16),
            lookup,
            preferred_element_type=jnp.float32,
        )
        for k in range(TOP)
    ]
    final_out = base_slice + gate_weights[:, 0:1] * picked[0] + gate_weights[:, 1:2] * picked[1]
    return final_out.astype(jnp.bfloat16)


def solution(mesh):
    in_specs = (
        P("ctx", "head"),
        P("ctx", "head"),
        P("ctx", "head"),
        P("head", "ctx"),
        P("ctx", None),
        P("head", "ctx"),
        P("head"),
        P(),
        P(),
        P("ctx", None, "head"),
        P("ctx", None, "head"),
        P("ctx", "head", None),
        P("ctx", None),
    )
    out_specs = P("ctx", "head")
    return jax.shard_map(body, mesh=mesh, in_specs=in_specs, out_specs=out_specs, check_vma=False)
```

```python
import jax
import jax.numpy as jnp
from jax import lax
from jax.sharding import PartitionSpec as P

TOP = 2


PRECISE = lax.Precision.HIGHEST


def prior_states(final_log, local_state, axis):
    peers = lax.axis_size(axis)
    heads_here, head_size = local_state.shape[0], local_state.shape[2]

    def pack(value):
        state, total = value
        high = total.astype(jnp.bfloat16)
        rest = total - high.astype(jnp.float32)
        middle = rest.astype(jnp.bfloat16)
        low = (rest - middle.astype(jnp.float32)).astype(jnp.bfloat16)
        extra = jnp.zeros((heads_here, 16, head_size), jnp.bfloat16)
        extra = extra.at[:, 0:3, 0].set(jnp.stack([high, middle, low], axis=1))
        return jnp.concatenate([state.astype(jnp.bfloat16), extra], axis=1)

    def unpack(packed):
        state = packed[:, :head_size].astype(jnp.float32)
        total = jnp.sum(packed[:, head_size : head_size + 3, 0].astype(jnp.float32), axis=1)
        return (state, total)

    def combine(earlier, later):
        return (
            jnp.exp(later[1])[:, None, None] * earlier[0] + later[0],
            earlier[1] + later[1],
        )

    def shifted(value, distance):
        pairs = [(k, k + distance) for k in range(peers - distance)]
        return unpack(lax.ppermute(pack(value), axis, pairs))

    own = (local_state, final_log)
    before = combine(shifted(own, 2), shifted(own, 1))
    distance = 2
    while distance < peers:
        before = combine(shifted(before, distance), before)
        distance *= 2
    return before[0]


def local_attention(query_block, key_block, value_block, decay_block):
    running = jnp.cumsum(decay_block, axis=1)
    length_here = decay_block.shape[1]
    row_index = lax.broadcasted_iota(jnp.int32, (length_here, length_here), 0)
    col_index = lax.broadcasted_iota(jnp.int32, (length_here, length_here), 1)
    causal = (col_index <= row_index)[None]
    spread = jnp.where(causal, running[:, :, None] - running[:, None, :], 0.0)
    decay_weights = jnp.where(causal, jnp.exp(spread), 0.0)
    scores = jnp.einsum("htd,hsd->hts", query_block, key_block, precision=PRECISE) * decay_weights
    inside_part = jnp.einsum("hts,hse->hte", scores, value_block, precision=PRECISE)
    final_log = running[:, -1]
    tail_decay = jnp.exp(final_log[:, None] - running)
    local_state = jnp.einsum(
        "hsd,hse->hde", key_block * tail_decay[:, :, None], value_block, precision=PRECISE
    )
    return (inside_part, running, local_state, final_log)


def route_tokens(logits, expert_ids, experts_total):
    onehot = expert_ids[:, :, None] == lax.broadcasted_iota(jnp.int32, (1, 1, experts_total), 2)
    chosen = jnp.sum(jnp.where(onehot, logits[:, None, :], 0.0), axis=2)
    leading = jax.nn.sigmoid(chosen[:, 0] - chosen[:, 1])
    gate_weights = jnp.stack([leading, 1.0 - leading], axis=1)
    marked = onehot.reshape(-1, experts_total).astype(jnp.int32)
    earlier = jnp.cumsum(marked, axis=0) - marked
    slot_index = jnp.sum(earlier * marked, axis=1).reshape(expert_ids.shape)
    return (gate_weights, slot_index)


def body(
    query_vectors,
    key_vectors,
    value_vectors,
    log_decay,
    residual,
    out_weight,
    attn_gain,
    moe_gain,
    router,
    w_gate,
    w_up,
    w_down,
    expert_ids,
):
    token_count = query_vectors.shape[0]
    heads_here = log_decay.shape[0]
    head_size = query_vectors.shape[1] // heads_here

    def split_heads(matrix_in):
        return (
            matrix_in.astype(jnp.float32)
            .reshape(token_count, heads_here, head_size)
            .transpose(1, 0, 2)
        )

    query_heads = split_heads(query_vectors)
    inside_part, running, local_state, final_log = local_attention(
        query_heads, split_heads(key_vectors), split_heads(value_vectors), log_decay
    )
    prior_state = prior_states(final_log, local_state, "ctx")
    outside_part = jnp.exp(running)[:, :, None] * jnp.einsum(
        "htd,hde->hte", query_heads, prior_state, precision=PRECISE
    )
    attended = inside_part + outside_part
    square_mean = jnp.mean(attended * attended, axis=2, keepdims=True)
    heads_normed = (
        attended * lax.rsqrt(square_mean + 1e-05) * attn_gain.reshape(heads_here, 1, head_size)
    )
    heads_normed = (
        heads_normed.astype(jnp.bfloat16)
        .transpose(1, 0, 2)
        .reshape(token_count, heads_here * head_size)
    )
    ctx_size = lax.axis_size("ctx")
    head_count = lax.axis_size("head")
    weight_blocks = lax.all_gather(out_weight, "ctx")
    model_width = residual.shape[1]
    experts_total = router.shape[1]
    capacity = 2 * token_count * TOP // experts_total
    slice_width = model_width // head_count
    slice_start = lax.axis_index("head") * slice_width
    partial_out = jnp.einsum(
        "tk,ckd->tcd", heads_normed, weight_blocks, preferred_element_type=jnp.float32
    ).reshape(token_count, head_count, slice_width)
    pieces = lax.all_to_all(
        partial_out.astype(jnp.bfloat16).transpose(1, 0, 2),
        "head",
        split_axis=0,
        concat_axis=0,
        tiled=True,
    )
    projected = jnp.sum(pieces.astype(jnp.float32), axis=0)
    own_residual = lax.dynamic_slice_in_dim(residual, slice_start, slice_width, 1)
    mixed_slice = (own_residual.astype(jnp.float32) + projected).astype(jnp.bfloat16)
    mixed_all = lax.all_to_all(
        jnp.broadcast_to(mixed_slice[None], (head_count,) + mixed_slice.shape),
        "head",
        split_axis=0,
        concat_axis=0,
        tiled=True,
    )
    mixed_rows = mixed_all.transpose(1, 0, 2).reshape(token_count, model_width)
    mixed_wide = mixed_rows.astype(jnp.float32)
    inv_rms = lax.rsqrt(jnp.mean(mixed_wide * mixed_wide, axis=1, keepdims=True) + 1e-06)
    scaled = mixed_wide * moe_gain[None, :]
    moe_in = (scaled * inv_rms).astype(jnp.bfloat16)
    logits = inv_rms * jnp.dot(scaled, router, precision=PRECISE)
    base_slice = lax.dynamic_slice_in_dim(mixed_wide, slice_start, slice_width, 1)
    gate_weights, slot_index = route_tokens(logits, expert_ids, experts_total)
    target = (expert_ids * capacity + slot_index).reshape(-1)
    width_here = moe_in.shape[1]
    slots = lax.broadcasted_iota(jnp.int32, (experts_total * capacity, token_count, TOP), 0)
    chosen = jnp.any(slots == target.reshape(token_count, TOP)[None], axis=2)
    packed = jnp.dot(
        chosen.astype(jnp.bfloat16), moe_in, preferred_element_type=jnp.float32
    ).astype(jnp.bfloat16)
    halves = packed.reshape(experts_total, 2, capacity // 2, width_here)
    partial_halves = []
    for half in range(2):
        arrived = lax.all_to_all(
            halves[:, half], "ctx", split_axis=0, concat_axis=0, tiled=True
        )
        flat_rows = arrived.reshape(-1, model_width)
        gate_part = jnp.dot(flat_rows, w_gate[0], preferred_element_type=jnp.float32)
        up_part = jnp.dot(flat_rows, w_up[0], preferred_element_type=jnp.float32)
        hidden = (jax.nn.silu(gate_part) * up_part).astype(jnp.bfloat16)
        partial_halves.append(
            jnp.dot(hidden, w_down[0], preferred_element_type=jnp.float32)
            .astype(jnp.bfloat16)
            .reshape(arrived.shape)
        )
    partial_down = jnp.stack(partial_halves, axis=1).reshape(-1, model_width)
    summed = lax.psum_scatter(partial_down, "head", scatter_dimension=1, tiled=True)
    returned = lax.all_to_all(
        summed.reshape(experts_total, capacity, slice_width),
        "ctx",
        split_axis=0,
        concat_axis=0,
        tiled=True,
    )
    lookup = returned.reshape(experts_total * capacity, slice_width)
    columns = lax.broadcasted_iota(jnp.int32, (token_count, experts_total * capacity), 1)
    ranked = target.reshape(token_count, TOP)
    picked = [
        jnp.dot(
            (columns == ranked[:, k : k + 1]).astype(jnp.bfloat16),
            lookup,
            preferred_element_type=jnp.float32,
        )
        for k in range(TOP)
    ]
    final_out = base_slice + gate_weights[:, 0:1] * picked[0] + gate_weights[:, 1:2] * picked[1]
    return final_out.astype(jnp.bfloat16)


def solution(mesh):
    in_specs = (
        P("ctx", "head"),
        P("ctx", "head"),
        P("ctx", "head"),
        P("head", "ctx"),
        P("ctx", None),
        P("head", "ctx"),
        P("head"),
        P(),
        P(),
        P("ctx", None, "head"),
        P("ctx", None, "head"),
        P("ctx", "head", None),
        P("ctx", None),
    )
    out_specs = P("ctx", "head")
    return jax.shard_map(body, mesh=mesh, in_specs=in_specs, out_specs=out_specs, check_vma=False)
```

```python
import jax
import jax.numpy as jnp
from jax import lax
from jax.sharding import PartitionSpec as P

TOP = 2


PRECISE = lax.Precision.HIGHEST


def prior_states(final_log, local_state, axis):
    peers = lax.axis_size(axis)
    heads_here, head_size = local_state.shape[0], local_state.shape[2]

    def pack(value):
        state, total = value
        high = total.astype(jnp.bfloat16)
        rest = total - high.astype(jnp.float32)
        middle = rest.astype(jnp.bfloat16)
        low = (rest - middle.astype(jnp.float32)).astype(jnp.bfloat16)
        extra = jnp.zeros((heads_here, 16, head_size), jnp.bfloat16)
        extra = extra.at[:, 0:3, 0].set(jnp.stack([high, middle, low], axis=1))
        return jnp.concatenate([state.astype(jnp.bfloat16), extra], axis=1)

    def unpack(packed):
        state = packed[:, :head_size].astype(jnp.float32)
        total = jnp.sum(packed[:, head_size : head_size + 3, 0].astype(jnp.float32), axis=1)
        return (state, total)

    def combine(earlier, later):
        return (
            jnp.exp(later[1])[:, None, None] * earlier[0] + later[0],
            earlier[1] + later[1],
        )

    def shifted(value, distance):
        pairs = [(k, k + distance) for k in range(peers - distance)]
        return unpack(lax.ppermute(pack(value), axis, pairs))

    own = (local_state, final_log)
    before = combine(shifted(own, 2), shifted(own, 1))
    distance = 2
    while distance < peers:
        before = combine(shifted(before, distance), before)
        distance *= 2
    return before[0]


def local_attention(query_block, key_block, value_block, decay_block):
    running = jnp.cumsum(decay_block, axis=1)
    length_here = decay_block.shape[1]
    row_index = lax.broadcasted_iota(jnp.int32, (length_here, length_here), 0)
    col_index = lax.broadcasted_iota(jnp.int32, (length_here, length_here), 1)
    causal = (col_index <= row_index)[None]
    spread = jnp.where(causal, running[:, :, None] - running[:, None, :], 0.0)
    decay_weights = jnp.where(causal, jnp.exp(spread), 0.0)
    scores = jnp.einsum("htd,hsd->hts", query_block, key_block, precision=PRECISE) * decay_weights
    inside_part = jnp.einsum("hts,hse->hte", scores, value_block, precision=PRECISE)
    final_log = running[:, -1]
    tail_decay = jnp.exp(final_log[:, None] - running)
    local_state = jnp.einsum(
        "hsd,hse->hde", key_block * tail_decay[:, :, None], value_block, precision=PRECISE
    )
    return (inside_part, running, local_state, final_log)


def route_tokens(logits, expert_ids, experts_total):
    onehot = expert_ids[:, :, None] == lax.broadcasted_iota(jnp.int32, (1, 1, experts_total), 2)
    chosen = jnp.sum(jnp.where(onehot, logits[:, None, :], 0.0), axis=2)
    leading = jax.nn.sigmoid(chosen[:, 0] - chosen[:, 1])
    gate_weights = jnp.stack([leading, 1.0 - leading], axis=1)
    marked = onehot.reshape(-1, experts_total).astype(jnp.int32)
    earlier = jnp.cumsum(marked, axis=0) - marked
    slot_index = jnp.sum(earlier * marked, axis=1).reshape(expert_ids.shape)
    return (gate_weights, slot_index)


def body(
    query_vectors,
    key_vectors,
    value_vectors,
    log_decay,
    residual,
    out_weight,
    attn_gain,
    moe_gain,
    router,
    w_gate,
    w_up,
    w_down,
    expert_ids,
):
    token_count = query_vectors.shape[0]
    heads_here = log_decay.shape[0]
    head_size = query_vectors.shape[1] // heads_here

    def split_heads(matrix_in):
        return (
            matrix_in.astype(jnp.float32)
            .reshape(token_count, heads_here, head_size)
            .transpose(1, 0, 2)
        )

    query_heads = split_heads(query_vectors)
    inside_part, running, local_state, final_log = local_attention(
        query_heads, split_heads(key_vectors), split_heads(value_vectors), log_decay
    )
    prior_state = prior_states(final_log, local_state, "ctx")
    outside_part = jnp.exp(running)[:, :, None] * jnp.einsum(
        "htd,hde->hte", query_heads, prior_state, precision=PRECISE
    )
    attended = inside_part + outside_part
    square_mean = jnp.mean(attended * attended, axis=2, keepdims=True)
    heads_normed = (
        attended * lax.rsqrt(square_mean + 1e-05) * attn_gain.reshape(heads_here, 1, head_size)
    )
    heads_normed = (
        heads_normed.astype(jnp.bfloat16)
        .transpose(1, 0, 2)
        .reshape(token_count, heads_here * head_size)
    )
    ctx_size = lax.axis_size("ctx")
    head_count = lax.axis_size("head")
    weight_blocks = lax.all_gather(out_weight, "ctx", axis=1, tiled=True)
    model_width = residual.shape[1]
    experts_total = router.shape[1]
    capacity = 2 * token_count * TOP // experts_total
    slice_width = model_width // head_count
    slice_start = lax.axis_index("head") * slice_width
    partial_out = jnp.dot(
        heads_normed, weight_blocks, preferred_element_type=jnp.float32
    ).reshape(token_count, head_count, slice_width)
    pieces = lax.all_to_all(
        partial_out.astype(jnp.bfloat16).transpose(1, 0, 2),
        "head",
        split_axis=0,
        concat_axis=0,
        tiled=True,
    )
    projected = jnp.sum(pieces.astype(jnp.float32), axis=0)
    own_residual = lax.dynamic_slice_in_dim(residual, slice_start, slice_width, 1)
    mixed_slice = (own_residual.astype(jnp.float32) + projected).astype(jnp.bfloat16)
    mixed_all = lax.all_to_all(
        jnp.broadcast_to(mixed_slice[None], (head_count,) + mixed_slice.shape),
        "head",
        split_axis=0,
        concat_axis=0,
        tiled=True,
    )
    mixed_rows = mixed_all.transpose(1, 0, 2).reshape(token_count, model_width)
    mixed_wide = mixed_rows.astype(jnp.float32)
    inv_rms = lax.rsqrt(jnp.mean(mixed_wide * mixed_wide, axis=1, keepdims=True) + 1e-06)
    scaled = mixed_wide * moe_gain[None, :]
    moe_in = (scaled * inv_rms).astype(jnp.bfloat16)
    logits = inv_rms * jnp.dot(scaled, router, precision=PRECISE)
    base_slice = lax.dynamic_slice_in_dim(mixed_wide, slice_start, slice_width, 1)
    gate_weights, slot_index = route_tokens(logits, expert_ids, experts_total)
    target = (expert_ids * capacity + slot_index).reshape(-1)
    width_here = moe_in.shape[1]
    slots = lax.broadcasted_iota(jnp.int32, (experts_total * capacity, token_count, TOP), 0)
    chosen = jnp.any(slots == target.reshape(token_count, TOP)[None], axis=2)
    packed = jnp.dot(
        chosen.astype(jnp.bfloat16), moe_in, preferred_element_type=jnp.float32
    ).astype(jnp.bfloat16)
    arrived = lax.all_to_all(
        packed.reshape(experts_total, capacity, width_here),
        "ctx",
        split_axis=0,
        concat_axis=0,
        tiled=True,
    )
    flat_rows = arrived.reshape(-1, model_width)
    gate_part = jnp.dot(flat_rows, w_gate[0], preferred_element_type=jnp.float32)
    up_part = jnp.dot(flat_rows, w_up[0], preferred_element_type=jnp.float32)
    hidden = (jax.nn.silu(gate_part) * up_part).astype(jnp.bfloat16)
    partial_down = jnp.dot(hidden, w_down[0], preferred_element_type=jnp.float32)
    summed = lax.psum_scatter(
        partial_down.astype(jnp.bfloat16), "head", scatter_dimension=1, tiled=True
    )
    returned = lax.all_to_all(
        summed.reshape(experts_total, capacity, slice_width),
        "ctx",
        split_axis=0,
        concat_axis=0,
        tiled=True,
    )
    lookup = returned.reshape(experts_total * capacity, slice_width)
    columns = lax.broadcasted_iota(jnp.int32, (token_count, experts_total * capacity), 1)
    ranked = target.reshape(token_count, TOP)
    picked = [
        jnp.dot(
            (columns == ranked[:, k : k + 1]).astype(jnp.bfloat16),
            lookup,
            preferred_element_type=jnp.float32,
        )
        for k in range(TOP)
    ]
    final_out = base_slice + gate_weights[:, 0:1] * picked[0] + gate_weights[:, 1:2] * picked[1]
    return final_out.astype(jnp.bfloat16)


def solution(mesh):
    in_specs = (
        P("ctx", "head"),
        P("ctx", "head"),
        P("ctx", "head"),
        P("head", "ctx"),
        P("ctx", None),
        P("head", "ctx"),
        P("head"),
        P(),
        P(),
        P("ctx", None, "head"),
        P("ctx", None, "head"),
        P("ctx", "head", None),
        P("ctx", None),
    )
    out_specs = P("ctx", "head")
    return jax.shard_map(body, mesh=mesh, in_specs=in_specs, out_specs=out_specs, check_vma=False)
```

```python
import jax
import jax.numpy as jnp
from jax import lax
from jax.sharding import PartitionSpec as P

TOP = 2


PRECISE = lax.Precision.HIGHEST


def prior_states(final_log, local_state, axis):
    peers = lax.axis_size(axis)
    heads_here, head_size = local_state.shape[0], local_state.shape[2]

    def pack(value):
        state, total = value
        high = total.astype(jnp.bfloat16)
        rest = total - high.astype(jnp.float32)
        middle = rest.astype(jnp.bfloat16)
        low = (rest - middle.astype(jnp.float32)).astype(jnp.bfloat16)
        extra = jnp.zeros((heads_here, 16, head_size), jnp.bfloat16)
        extra = extra.at[:, 0:3, 0].set(jnp.stack([high, middle, low], axis=1))
        return jnp.concatenate([state.astype(jnp.bfloat16), extra], axis=1)

    def unpack(packed):
        state = packed[:, :head_size].astype(jnp.float32)
        total = jnp.sum(packed[:, head_size : head_size + 3, 0].astype(jnp.float32), axis=1)
        return (state, total)

    def combine(earlier, later):
        return (
            jnp.exp(later[1])[:, None, None] * earlier[0] + later[0],
            earlier[1] + later[1],
        )

    def shifted(value, distance):
        pairs = [(k, k + distance) for k in range(peers - distance)]
        return unpack(lax.ppermute(pack(value), axis, pairs))

    own = (local_state, final_log)
    before = combine(shifted(own, 2), shifted(own, 1))
    distance = 2
    while distance < peers:
        before = combine(shifted(before, distance), before)
        distance *= 2
    return before[0]


def local_attention(query_block, key_block, value_block, decay_block):
    running = jnp.cumsum(decay_block, axis=1)
    length_here = decay_block.shape[1]
    row_index = lax.broadcasted_iota(jnp.int32, (length_here, length_here), 0)
    col_index = lax.broadcasted_iota(jnp.int32, (length_here, length_here), 1)
    causal = (col_index <= row_index)[None]
    spread = jnp.where(causal, running[:, :, None] - running[:, None, :], 0.0)
    decay_weights = jnp.where(causal, jnp.exp(spread), 0.0)
    scores = jnp.einsum("htd,hsd->hts", query_block, key_block, precision=PRECISE) * decay_weights
    inside_part = jnp.einsum("hts,hse->hte", scores, value_block, precision=PRECISE)
    final_log = running[:, -1]
    tail_decay = jnp.exp(final_log[:, None] - running)
    local_state = jnp.einsum(
        "hsd,hse->hde", key_block * tail_decay[:, :, None], value_block, precision=PRECISE
    )
    return (inside_part, running, local_state, final_log)


def route_tokens(logits, expert_ids, experts_total):
    onehot = expert_ids[:, :, None] == lax.broadcasted_iota(jnp.int32, (1, 1, experts_total), 2)
    chosen = jnp.sum(jnp.where(onehot, logits[:, None, :], 0.0), axis=2)
    leading = jax.nn.sigmoid(chosen[:, 0] - chosen[:, 1])
    gate_weights = jnp.stack([leading, 1.0 - leading], axis=1)
    marked = onehot.reshape(-1, experts_total).astype(jnp.int32)
    earlier = jnp.cumsum(marked, axis=0) - marked
    slot_index = jnp.sum(earlier * marked, axis=1).reshape(expert_ids.shape)
    return (gate_weights, slot_index)


def body(
    query_vectors,
    key_vectors,
    value_vectors,
    log_decay,
    residual,
    out_weight,
    attn_gain,
    moe_gain,
    router,
    w_gate,
    w_up,
    w_down,
    expert_ids,
):
    token_count = query_vectors.shape[0]
    heads_here = log_decay.shape[0]
    head_size = query_vectors.shape[1] // heads_here

    def split_heads(matrix_in):
        return (
            matrix_in.astype(jnp.float32)
            .reshape(token_count, heads_here, head_size)
            .transpose(1, 0, 2)
        )

    query_heads = split_heads(query_vectors)
    inside_part, running, local_state, final_log = local_attention(
        query_heads, split_heads(key_vectors), split_heads(value_vectors), log_decay
    )
    prior_state = prior_states(final_log, local_state, "ctx")
    outside_part = jnp.exp(running)[:, :, None] * jnp.einsum(
        "htd,hde->hte", query_heads, prior_state, precision=PRECISE
    )
    attended = inside_part + outside_part
    square_mean = jnp.mean(attended * attended, axis=2, keepdims=True)
    heads_normed = (
        attended * lax.rsqrt(square_mean + 1e-05) * attn_gain.reshape(heads_here, 1, head_size)
    )
    heads_normed = (
        heads_normed.astype(jnp.bfloat16)
        .transpose(1, 0, 2)
        .reshape(token_count, heads_here * head_size)
    )
    ctx_size = lax.axis_size("ctx")
    head_count = lax.axis_size("head")
    weight_blocks = lax.all_gather(out_weight, "ctx")
    model_width = residual.shape[1]
    experts_total = router.shape[1]
    capacity = 2 * token_count * TOP // experts_total
    slice_width = model_width // head_count
    slice_start = lax.axis_index("head") * slice_width
    partial_out = jnp.einsum(
        "tk,ckd->tcd", heads_normed, weight_blocks, preferred_element_type=jnp.float32
    ).reshape(token_count, head_count, slice_width)
    pieces = lax.all_to_all(
        partial_out.astype(jnp.bfloat16).transpose(1, 0, 2),
        "head",
        split_axis=0,
        concat_axis=0,
        tiled=True,
    )
    projected = jnp.sum(pieces.astype(jnp.float32), axis=0)
    own_residual = lax.dynamic_slice_in_dim(residual, slice_start, slice_width, 1)
    mixed_slice = (own_residual.astype(jnp.float32) + projected).astype(jnp.bfloat16)
    mixed_all = lax.all_to_all(
        jnp.broadcast_to(mixed_slice[None], (head_count,) + mixed_slice.shape),
        "head",
        split_axis=0,
        concat_axis=0,
        tiled=True,
    )
    mixed_rows = mixed_all.transpose(1, 0, 2).reshape(token_count, model_width)
    mixed_wide = mixed_rows.astype(jnp.float32)
    inv_rms = lax.rsqrt(jnp.mean(mixed_wide * mixed_wide, axis=1, keepdims=True) + 1e-06)
    scaled = mixed_wide * moe_gain[None, :]
    moe_in = (scaled * inv_rms).astype(jnp.bfloat16)
    logits = inv_rms * jnp.dot(scaled, router, precision=PRECISE)
    base_slice = lax.dynamic_slice_in_dim(mixed_wide, slice_start, slice_width, 1)
    gate_weights, slot_index = route_tokens(logits, expert_ids, experts_total)
    target = (expert_ids * capacity + slot_index).reshape(-1)
    width_here = moe_in.shape[1]
    slots = lax.broadcasted_iota(jnp.int32, (experts_total * capacity, token_count, TOP), 0)
    chosen = jnp.any(slots == target.reshape(token_count, TOP)[None], axis=2)
    packed = jnp.dot(
        chosen.astype(jnp.bfloat16), moe_in, preferred_element_type=jnp.float32
    ).astype(jnp.bfloat16)
    arrived = lax.all_to_all(
        packed.reshape(experts_total, capacity, width_here),
        "ctx",
        split_axis=0,
        concat_axis=0,
        tiled=True,
    )
    flat_rows = arrived.reshape(-1, model_width)
    gate_part = jnp.dot(flat_rows, w_gate[0], preferred_element_type=jnp.float32)
    up_part = jnp.dot(flat_rows, w_up[0], preferred_element_type=jnp.float32)
    hidden = (jax.nn.silu(gate_part) * up_part).astype(jnp.bfloat16)
    partial_down = jnp.einsum(
        "sf,fhj->hsj",
        hidden,
        w_down[0].reshape(w_down.shape[1], head_count, slice_width),
        preferred_element_type=jnp.float32,
    )
    summed = lax.psum_scatter(
        partial_down.astype(jnp.bfloat16), "head", scatter_dimension=0, tiled=True
    ).reshape(-1, slice_width)
    returned = lax.all_to_all(
        summed.reshape(experts_total, capacity, slice_width),
        "ctx",
        split_axis=0,
        concat_axis=0,
        tiled=True,
    )
    lookup = returned.reshape(experts_total * capacity, slice_width)
    columns = lax.broadcasted_iota(jnp.int32, (token_count, experts_total * capacity), 1)
    ranked = target.reshape(token_count, TOP)
    picked = [
        jnp.dot(
            (columns == ranked[:, k : k + 1]).astype(jnp.bfloat16),
            lookup,
            preferred_element_type=jnp.float32,
        )
        for k in range(TOP)
    ]
    final_out = base_slice + gate_weights[:, 0:1] * picked[0] + gate_weights[:, 1:2] * picked[1]
    return final_out.astype(jnp.bfloat16)


def solution(mesh):
    in_specs = (
        P("ctx", "head"),
        P("ctx", "head"),
        P("ctx", "head"),
        P("head", "ctx"),
        P("ctx", None),
        P("head", "ctx"),
        P("head"),
        P(),
        P(),
        P("ctx", None, "head"),
        P("ctx", None, "head"),
        P("ctx", "head", None),
        P("ctx", None),
    )
    out_specs = P("ctx", "head")
    return jax.shard_map(body, mesh=mesh, in_specs=in_specs, out_specs=out_specs, check_vma=False)
```

```python
import jax
import jax.numpy as jnp
from jax import lax
from jax.sharding import PartitionSpec as P

TOP = 2


PRECISE = lax.Precision.HIGHEST


def prior_states(final_log, local_state, axis):
    peers = lax.axis_size(axis)
    heads_here, head_size = local_state.shape[0], local_state.shape[2]

    def pack(value):
        state, total = value
        high = total.astype(jnp.bfloat16)
        rest = total - high.astype(jnp.float32)
        middle = rest.astype(jnp.bfloat16)
        low = (rest - middle.astype(jnp.float32)).astype(jnp.bfloat16)
        extra = jnp.zeros((heads_here, 16, head_size), jnp.bfloat16)
        extra = extra.at[:, 0:3, 0].set(jnp.stack([high, middle, low], axis=1))
        return jnp.concatenate([state.astype(jnp.bfloat16), extra], axis=1)

    def unpack(packed):
        state = packed[:, :head_size].astype(jnp.float32)
        total = jnp.sum(packed[:, head_size : head_size + 3, 0].astype(jnp.float32), axis=1)
        return (state, total)

    def combine(earlier, later):
        return (
            jnp.exp(later[1])[:, None, None] * earlier[0] + later[0],
            earlier[1] + later[1],
        )

    def shifted(value, distance):
        pairs = [(k, k + distance) for k in range(peers - distance)]
        return unpack(lax.ppermute(pack(value), axis, pairs))

    own = (local_state, final_log)
    before = combine(shifted(own, 2), shifted(own, 1))
    distance = 2
    while distance < peers:
        before = combine(shifted(before, distance), before)
        distance *= 2
    return before[0]


def local_attention(query_block, key_block, value_block, decay_block):
    running = jnp.cumsum(decay_block, axis=1)
    length_here = decay_block.shape[1]
    row_index = lax.broadcasted_iota(jnp.int32, (length_here, length_here), 0)
    col_index = lax.broadcasted_iota(jnp.int32, (length_here, length_here), 1)
    causal = (col_index <= row_index)[None]
    spread = jnp.where(causal, running[:, :, None] - running[:, None, :], 0.0)
    decay_weights = jnp.where(causal, jnp.exp(spread), 0.0)
    scores = jnp.einsum("htd,hsd->hts", query_block, key_block, precision=PRECISE) * decay_weights
    inside_part = jnp.einsum("hts,hse->hte", scores, value_block, precision=PRECISE)
    final_log = running[:, -1]
    tail_decay = jnp.exp(final_log[:, None] - running)
    local_state = jnp.einsum(
        "hsd,hse->hde", key_block * tail_decay[:, :, None], value_block, precision=PRECISE
    )
    return (inside_part, running, local_state, final_log)


def route_tokens(logits, expert_ids, experts_total):
    onehot = expert_ids[:, :, None] == lax.broadcasted_iota(jnp.int32, (1, 1, experts_total), 2)
    chosen = jnp.sum(jnp.where(onehot, logits[:, None, :], 0.0), axis=2)
    leading = jax.nn.sigmoid(chosen[:, 0] - chosen[:, 1])
    gate_weights = jnp.stack([leading, 1.0 - leading], axis=1)
    marked = onehot.reshape(-1, experts_total).astype(jnp.int32)
    earlier = jnp.cumsum(marked, axis=0) - marked
    slot_index = jnp.sum(earlier * marked, axis=1).reshape(expert_ids.shape)
    return (gate_weights, slot_index)


def body(
    query_vectors,
    key_vectors,
    value_vectors,
    log_decay,
    residual,
    out_weight,
    attn_gain,
    moe_gain,
    router,
    w_gate,
    w_up,
    w_down,
    expert_ids,
):
    token_count = query_vectors.shape[0]
    heads_here = log_decay.shape[0]
    head_size = query_vectors.shape[1] // heads_here

    def split_heads(matrix_in):
        return (
            matrix_in.astype(jnp.float32)
            .reshape(token_count, heads_here, head_size)
            .transpose(1, 0, 2)
        )

    query_heads = split_heads(query_vectors)
    inside_part, running, local_state, final_log = local_attention(
        query_heads, split_heads(key_vectors), split_heads(value_vectors), log_decay
    )
    prior_state = prior_states(final_log, local_state, "ctx")
    outside_part = jnp.exp(running)[:, :, None] * jnp.einsum(
        "htd,hde->hte", query_heads, prior_state, precision=PRECISE
    )
    attended = inside_part + outside_part
    square_mean = jnp.mean(attended * attended, axis=2, keepdims=True)
    heads_normed = (
        attended * lax.rsqrt(square_mean + 1e-05) * attn_gain.reshape(heads_here, 1, head_size)
    )
    heads_normed = (
        heads_normed.astype(jnp.bfloat16)
        .transpose(1, 0, 2)
        .reshape(token_count, heads_here * head_size)
    )
    ctx_size = lax.axis_size("ctx")
    head_count = lax.axis_size("head")
    weight_blocks = lax.all_gather(out_weight, "ctx")
    model_width = residual.shape[1]
    experts_total = router.shape[1]
    capacity = 2 * token_count * TOP // experts_total
    slice_width = model_width // head_count
    slice_start = lax.axis_index("head") * slice_width
    partial_out = jnp.einsum(
        "tk,ckd->tcd", heads_normed, weight_blocks, preferred_element_type=jnp.float32
    ).reshape(token_count, head_count, slice_width)
    pieces = lax.all_to_all(
        partial_out.astype(jnp.bfloat16).transpose(1, 0, 2),
        "head",
        split_axis=0,
        concat_axis=0,
        tiled=True,
    )
    projected = jnp.sum(pieces.astype(jnp.float32), axis=0)
    own_residual = lax.dynamic_slice_in_dim(residual, slice_start, slice_width, 1)
    mixed_slice = (own_residual.astype(jnp.float32) + projected).astype(jnp.bfloat16)
    mixed_all = lax.all_to_all(
        jnp.broadcast_to(mixed_slice[None], (head_count,) + mixed_slice.shape),
        "head",
        split_axis=0,
        concat_axis=0,
        tiled=True,
    )
    mixed_rows = mixed_all.transpose(1, 0, 2).reshape(token_count, model_width)
    mixed_wide = mixed_rows.astype(jnp.float32)
    inv_rms = lax.rsqrt(jnp.mean(mixed_wide * mixed_wide, axis=1, keepdims=True) + 1e-06)
    scaled = mixed_wide * moe_gain[None, :]
    moe_in = (scaled * inv_rms).astype(jnp.bfloat16)
    logits = inv_rms * jnp.dot(scaled, router, precision=PRECISE)
    base_slice = lax.dynamic_slice_in_dim(mixed_wide, slice_start, slice_width, 1)
    gate_weights, slot_index = route_tokens(logits, expert_ids, experts_total)
    target = (expert_ids * capacity + slot_index).reshape(-1)
    width_here = moe_in.shape[1]
    slots = lax.broadcasted_iota(jnp.int32, (experts_total * capacity, token_count, TOP), 0)
    chosen = jnp.any(slots == target.reshape(token_count, TOP)[None], axis=2)
    packed = jnp.dot(
        chosen.astype(jnp.bfloat16), moe_in, preferred_element_type=jnp.float32
    ).astype(jnp.bfloat16)
    arrived = lax.all_to_all(
        packed.reshape(experts_total, capacity, width_here),
        "ctx",
        split_axis=0,
        concat_axis=0,
        tiled=True,
    )
    flat_rows = arrived.reshape(-1, model_width)
    gate_part = jnp.dot(flat_rows, w_gate[0], preferred_element_type=jnp.float32)
    up_part = jnp.dot(flat_rows, w_up[0], preferred_element_type=jnp.float32)
    hidden = (jax.nn.silu(gate_part) * up_part).astype(jnp.bfloat16)
    partial_down = jnp.stack(
        [
            jnp.dot(
                hidden,
                w_down[0][:, group * slice_width : (group + 1) * slice_width],
                preferred_element_type=jnp.float32,
            )
            for group in range(head_count)
        ]
    )
    summed = lax.psum_scatter(
        partial_down.astype(jnp.bfloat16), "head", scatter_dimension=0, tiled=True
    ).reshape(-1, slice_width)
    returned = lax.all_to_all(
        summed.reshape(experts_total, capacity, slice_width),
        "ctx",
        split_axis=0,
        concat_axis=0,
        tiled=True,
    )
    lookup = returned.reshape(experts_total * capacity, slice_width)
    columns = lax.broadcasted_iota(jnp.int32, (token_count, experts_total * capacity), 1)
    ranked = target.reshape(token_count, TOP)
    picked = [
        jnp.dot(
            (columns == ranked[:, k : k + 1]).astype(jnp.bfloat16),
            lookup,
            preferred_element_type=jnp.float32,
        )
        for k in range(TOP)
    ]
    final_out = base_slice + gate_weights[:, 0:1] * picked[0] + gate_weights[:, 1:2] * picked[1]
    return final_out.astype(jnp.bfloat16)


def solution(mesh):
    in_specs = (
        P("ctx", "head"),
        P("ctx", "head"),
        P("ctx", "head"),
        P("head", "ctx"),
        P("ctx", None),
        P("head", "ctx"),
        P("head"),
        P(),
        P(),
        P("ctx", None, "head"),
        P("ctx", None, "head"),
        P("ctx", "head", None),
        P("ctx", None),
    )
    out_specs = P("ctx", "head")
    return jax.shard_map(body, mesh=mesh, in_specs=in_specs, out_specs=out_specs, check_vma=False)
```

```python
import jax
import jax.numpy as jnp
from jax import lax
from jax.sharding import PartitionSpec as P

TOP = 2


PRECISE = lax.Precision.HIGHEST


def prior_states(final_log, local_state, axis):
    peers = lax.axis_size(axis)
    heads_here, head_size = local_state.shape[0], local_state.shape[2]

    def pack(value):
        state, total = value
        high = total.astype(jnp.bfloat16)
        rest = total - high.astype(jnp.float32)
        middle = rest.astype(jnp.bfloat16)
        low = (rest - middle.astype(jnp.float32)).astype(jnp.bfloat16)
        extra = jnp.zeros((heads_here, 16, head_size), jnp.bfloat16)
        extra = extra.at[:, 0:3, 0].set(jnp.stack([high, middle, low], axis=1))
        return jnp.concatenate([state.astype(jnp.bfloat16), extra], axis=1)

    def unpack(packed):
        state = packed[:, :head_size].astype(jnp.float32)
        total = jnp.sum(packed[:, head_size : head_size + 3, 0].astype(jnp.float32), axis=1)
        return (state, total)

    def combine(earlier, later):
        return (
            jnp.exp(later[1])[:, None, None] * earlier[0] + later[0],
            earlier[1] + later[1],
        )

    def shifted(value, distance):
        pairs = [(k, k + distance) for k in range(peers - distance)]
        return unpack(lax.ppermute(pack(value), axis, pairs))

    own = (local_state, final_log)
    before = combine(shifted(own, 2), shifted(own, 1))
    distance = 2
    while distance < peers:
        before = combine(shifted(before, distance), before)
        distance *= 2
    return before[0]


def local_attention(query_block, key_block, value_block, decay_block):
    running = jnp.cumsum(decay_block, axis=1)
    length_here = decay_block.shape[1]
    row_index = lax.broadcasted_iota(jnp.int32, (length_here, length_here), 0)
    col_index = lax.broadcasted_iota(jnp.int32, (length_here, length_here), 1)
    causal = (col_index <= row_index)[None]
    spread = jnp.where(causal, running[:, :, None] - running[:, None, :], 0.0)
    decay_weights = jnp.where(causal, jnp.exp(spread), 0.0)
    scores = jnp.einsum("htd,hsd->hts", query_block, key_block, precision=PRECISE) * decay_weights
    inside_part = jnp.einsum("hts,hse->hte", scores, value_block, precision=PRECISE)
    final_log = running[:, -1]
    tail_decay = jnp.exp(final_log[:, None] - running)
    local_state = jnp.einsum(
        "hsd,hse->hde", key_block * tail_decay[:, :, None], value_block, precision=PRECISE
    )
    return (inside_part, running, local_state, final_log)


def route_tokens(logits, expert_ids, experts_total):
    onehot = expert_ids[:, :, None] == lax.broadcasted_iota(jnp.int32, (1, 1, experts_total), 2)
    chosen = jnp.sum(jnp.where(onehot, logits[:, None, :], 0.0), axis=2)
    leading = jax.nn.sigmoid(chosen[:, 0] - chosen[:, 1])
    gate_weights = jnp.stack([leading, 1.0 - leading], axis=1)
    marked = onehot.reshape(-1, experts_total).astype(jnp.int32)
    earlier = jnp.cumsum(marked, axis=0) - marked
    slot_index = jnp.sum(earlier * marked, axis=1).reshape(expert_ids.shape)
    return (gate_weights, slot_index)


def body(
    query_vectors,
    key_vectors,
    value_vectors,
    log_decay,
    residual,
    out_weight,
    attn_gain,
    moe_gain,
    router,
    w_gate,
    w_up,
    w_down,
    expert_ids,
):
    token_count = query_vectors.shape[0]
    heads_here = log_decay.shape[0]
    head_size = query_vectors.shape[1] // heads_here

    def split_heads(matrix_in):
        return (
            matrix_in.astype(jnp.float32)
            .reshape(token_count, heads_here, head_size)
            .transpose(1, 0, 2)
        )

    query_heads = split_heads(query_vectors)
    inside_part, running, local_state, final_log = local_attention(
        query_heads, split_heads(key_vectors), split_heads(value_vectors), log_decay
    )
    prior_state = prior_states(final_log, local_state, "ctx")
    outside_part = jnp.exp(running)[:, :, None] * jnp.einsum(
        "htd,hde->hte", query_heads, prior_state, precision=PRECISE
    )
    attended = inside_part + outside_part
    square_mean = jnp.mean(attended * attended, axis=2, keepdims=True)
    heads_normed = (
        attended * lax.rsqrt(square_mean + 1e-05) * attn_gain.reshape(heads_here, 1, head_size)
    )
    heads_normed = (
        heads_normed.astype(jnp.bfloat16)
        .transpose(1, 0, 2)
        .reshape(token_count, heads_here * head_size)
    )
    ctx_size = lax.axis_size("ctx")
    head_count = lax.axis_size("head")
    weight_blocks = lax.all_gather(out_weight, "ctx", axis=1, tiled=True)
    model_width = residual.shape[1]
    experts_total = router.shape[1]
    capacity = 2 * token_count * TOP // experts_total
    slice_width = model_width // head_count
    slice_start = lax.axis_index("head") * slice_width
    partial_out = jnp.stack(
        [
            jnp.dot(
                heads_normed,
                weight_blocks[:, group * slice_width : (group + 1) * slice_width],
                preferred_element_type=jnp.float32,
            )
            for group in range(head_count)
        ]
    )
    pieces = lax.all_to_all(
        partial_out.astype(jnp.bfloat16),
        "head",
        split_axis=0,
        concat_axis=0,
        tiled=True,
    )
    projected = jnp.sum(pieces.astype(jnp.float32), axis=0)
    own_residual = lax.dynamic_slice_in_dim(residual, slice_start, slice_width, 1)
    mixed_slice = (own_residual.astype(jnp.float32) + projected).astype(jnp.bfloat16)
    mixed_all = lax.all_to_all(
        jnp.broadcast_to(mixed_slice[None], (head_count,) + mixed_slice.shape),
        "head",
        split_axis=0,
        concat_axis=0,
        tiled=True,
    )
    mixed_rows = mixed_all.transpose(1, 0, 2).reshape(token_count, model_width)
    mixed_wide = mixed_rows.astype(jnp.float32)
    inv_rms = lax.rsqrt(jnp.mean(mixed_wide * mixed_wide, axis=1, keepdims=True) + 1e-06)
    scaled = mixed_wide * moe_gain[None, :]
    moe_in = (scaled * inv_rms).astype(jnp.bfloat16)
    logits = inv_rms * jnp.dot(scaled, router, precision=PRECISE)
    base_slice = lax.dynamic_slice_in_dim(mixed_wide, slice_start, slice_width, 1)
    gate_weights, slot_index = route_tokens(logits, expert_ids, experts_total)
    target = (expert_ids * capacity + slot_index).reshape(-1)
    width_here = moe_in.shape[1]
    slots = lax.broadcasted_iota(jnp.int32, (experts_total * capacity, token_count, TOP), 0)
    chosen = jnp.any(slots == target.reshape(token_count, TOP)[None], axis=2)
    packed = jnp.dot(
        chosen.astype(jnp.bfloat16), moe_in, preferred_element_type=jnp.float32
    ).astype(jnp.bfloat16)
    arrived = lax.all_to_all(
        packed.reshape(experts_total, capacity, width_here),
        "ctx",
        split_axis=0,
        concat_axis=0,
        tiled=True,
    )
    flat_rows = arrived.reshape(-1, model_width)
    gate_part = jnp.dot(flat_rows, w_gate[0], preferred_element_type=jnp.float32)
    up_part = jnp.dot(flat_rows, w_up[0], preferred_element_type=jnp.float32)
    hidden = (jax.nn.silu(gate_part) * up_part).astype(jnp.bfloat16)
    partial_down = jnp.stack(
        [
            jnp.dot(
                hidden,
                w_down[0][:, group * slice_width : (group + 1) * slice_width],
                preferred_element_type=jnp.float32,
            )
            for group in range(head_count)
        ]
    )
    summed = lax.psum_scatter(
        partial_down.astype(jnp.bfloat16), "head", scatter_dimension=0, tiled=True
    ).reshape(-1, slice_width)
    returned = lax.all_to_all(
        summed.reshape(experts_total, capacity, slice_width),
        "ctx",
        split_axis=0,
        concat_axis=0,
        tiled=True,
    )
    lookup = returned.reshape(experts_total * capacity, slice_width)
    columns = lax.broadcasted_iota(jnp.int32, (token_count, experts_total * capacity), 1)
    ranked = target.reshape(token_count, TOP)
    picked = [
        jnp.dot(
            (columns == ranked[:, k : k + 1]).astype(jnp.bfloat16),
            lookup,
            preferred_element_type=jnp.float32,
        )
        for k in range(TOP)
    ]
    final_out = base_slice + gate_weights[:, 0:1] * picked[0] + gate_weights[:, 1:2] * picked[1]
    return final_out.astype(jnp.bfloat16)


def solution(mesh):
    in_specs = (
        P("ctx", "head"),
        P("ctx", "head"),
        P("ctx", "head"),
        P("head", "ctx"),
        P("ctx", None),
        P("head", "ctx"),
        P("head"),
        P(),
        P(),
        P("ctx", None, "head"),
        P("ctx", None, "head"),
        P("ctx", "head", None),
        P("ctx", None),
    )
    out_specs = P("ctx", "head")
    return jax.shard_map(body, mesh=mesh, in_specs=in_specs, out_specs=out_specs, check_vma=False)
```
